1024 devices in a mesh: space: 128 (over z, y_hi, x), chan: 4 (over y_lo), dp: 2 (over core).
Axes of the slice: x: 8, y: 8 (y_hi: 2, y_lo: 4; y = y_hi * 4 + y_lo), z: 8, core: 2. Of those that a mesh axis runs over, the one named last changes fastest.
Arguments:
- volume: bfloat16 [2, 256, 16, 128, 256], P('dp', 'space', None, 'chan'), may hold values from -6 to 6
- kernel: bfloat16 [27, 128, 128], P(None, 'chan'), may hold values from -0.109375 to 0.109375
- cotangent: bfloat16 [2, 128, 8, 128, 128], P('dp', 'space', None, 'chan'), may hold values from -12 to 12
Outputs:
- response: bfloat16 [2, 128, 8, 128, 128], P('dp', 'space', None, 'chan')
- volume_grad: bfloat16 [2, 256, 16, 128, 256], P('dp', 'space', None, 'chan')
The draws below stay inside these ranges and needn't reach their ends.
All inputs are finite; a program needn't handle non-finite values.
Results may differ from the reference program's by a relative error of at most 0.001.
Values may be sent and summed in bfloat16 or wider, within the bound.
No kernel may reach another device: no remote copies, remote signals or barrier semaphores. Data moves between devices by JAX's collectives and lax.ppermute only.
A program may use at most 32 MiB of HBM per device.

```python
import jax
import jax.numpy as jnp
from jax import lax

C_IN = 128
C_OUT = 128
HEIGHT = 16
WIDTH = 256
TAPS = 27
BATCH = 2
DEPTH = 256
OUT_DEPTH = 128
OUT_H = 8
OUT_W = 128


def steps_of(own_key, shape, shards, low, top_value):
    def one(axis_at, blocks):
        draws = jax.random.uniform(jax.random.fold_in(jax.random.fold_in(own_key, 6), axis_at), (blocks,), jnp.float32, low / len(shards), top_value / len(shards))
        return jnp.repeat(jnp.exp(draws), shape[axis_at] // blocks).reshape((-1,) + (1,) * (len(shape) - axis_at - 1))

    loudness = one(*shards[0])
    for cut in shards[1:]:
        loudness = loudness * one(*cut)
    return loudness


def bell_draw(key, shape, scale, reach, pieces=(), kind=jnp.bfloat16):
    entries = scale * jax.random.normal(key, shape, jnp.float32)
    if pieces:
        entries = entries * steps_of(key, shape, pieces, -0.22, 0.18)
    return jnp.clip(entries, -reach, reach).astype(kind)


def setup_inputs(seed: int = 0) -> dict:
    splits = jax.random.split(jax.random.key(seed), 4)
    return {
        "volume": bell_draw(splits[0], (BATCH, DEPTH, HEIGHT, C_IN, WIDTH), 1.0, 6.0, ((0, 2), (1, 128), (3, 4))),
        "kernel": bell_draw(splits[1], (TAPS, C_IN, C_OUT), (TAPS * C_IN) ** -0.5, 0.109375, ((1, 4),)),
        "cotangent": bell_draw(splits[2], (BATCH, OUT_DEPTH, OUT_H, C_OUT, OUT_W), 2.0, 12.0, ((0, 2), (1, 128), (3, 4))),
    }


def transposed_plane(source, taps):
    count, planes, rows_out, cols_out, chans_out = source.shape
    chans_in = taps.shape[2]
    zero_row = jnp.zeros_like(source[:, :, :1])
    shift_row = jnp.concatenate([source[:, :, 1:], zero_row], axis=2)
    zero_col = jnp.zeros_like(source[:, :, :, :1])
    shift_col = jnp.concatenate([source[:, :, :, 1:], zero_col], axis=3)
    shift_both = jnp.concatenate([shift_row[:, :, :, 1:], jnp.zeros_like(shift_row[:, :, :, :1])], axis=3)
    sources = {(0, 0): source, (1, 0): shift_row, (0, 1): shift_col, (1, 1): shift_both}
    phases = {}
    for row_tap in range(3):
        for col_tap in range(3):
            picked = sources[(int(row_tap == 0), int(col_tap == 0))]
            weight = taps[row_tap, col_tap].astype(jnp.float32)
            term = jnp.einsum("bdhwe,ce->bdhwc", picked.astype(jnp.float32), weight)
            place = (0 if row_tap == 1 else 1, 0 if col_tap == 1 else 1)
            phases[place] = term if place not in phases else phases[place] + term
    upper = jnp.stack([phases[(0, 0)], phases[(0, 1)]], axis=4).reshape(count, planes, rows_out, 2 * cols_out, chans_in)
    lower = jnp.stack([phases[(1, 0)], phases[(1, 1)]], axis=4).reshape(count, planes, rows_out, 2 * cols_out, chans_in)
    return jnp.stack([upper, lower], axis=3).reshape(count, planes, 2 * rows_out, 2 * cols_out, chans_in)


def channels_last(volume, kernel, cotangent):
    count = volume.shape[0]
    padded = jnp.pad(volume, ((0, 0), (1, 0), (1, 0), (1, 0), (0, 0)))
    kernel_wide = kernel.astype(jnp.float32)

    def one_output(plane_out):
        block = lax.dynamic_slice_in_dim(padded, 2 * plane_out, 3, 1).astype(jnp.float32)
        total = jnp.zeros((count, 1, OUT_H, OUT_W, C_OUT), jnp.float32)
        for depth_tap in range(3):
            for row_tap in range(3):
                for col_tap in range(3):
                    piece = lax.slice(block, (0, depth_tap, row_tap, col_tap, 0),
                                      (count, depth_tap + 1, row_tap + 2 * OUT_H - 1, col_tap + 2 * OUT_W - 1, C_IN),
                                      (1, 1, 2, 2, 1))
                    index = 9 * depth_tap + 3 * row_tap + col_tap
                    total = total + jnp.einsum("bdhwc,ce->bdhwe", piece, kernel_wide[index])
        return total[:, 0].astype(jnp.bfloat16)

    response = jnp.moveaxis(lax.map(one_output, jnp.arange(OUT_DEPTH, dtype=jnp.int32)), 0, 1)

    extended = jnp.concatenate([cotangent, jnp.zeros_like(cotangent[:, :1])], axis=1)
    taps = kernel.reshape(3, 3, 3, C_IN, C_OUT)

    def one_input(plane_pair):
        current = lax.dynamic_slice_in_dim(extended, plane_pair, 1, 1)
        following = lax.dynamic_slice_in_dim(extended, plane_pair + 1, 1, 1)
        even_plane = transposed_plane(current, taps[1])
        odd_plane = transposed_plane(following, taps[0]) + transposed_plane(current, taps[2])
        return jnp.stack([even_plane[:, 0], odd_plane[:, 0]], axis=1).astype(jnp.bfloat16)

    pairs = lax.map(one_input, jnp.arange(OUT_DEPTH, dtype=jnp.int32))
    volume_grad = jnp.moveaxis(pairs, 0, 1).reshape(count, DEPTH, HEIGHT, WIDTH, C_IN)
    return response, volume_grad


def reference(volume, kernel, cotangent):
    response, volume_grad = channels_last(jnp.swapaxes(volume, 3, 4), kernel, jnp.swapaxes(cotangent, 3, 4))
    return jnp.swapaxes(response, 3, 4), jnp.swapaxes(volume_grad, 3, 4)
```

```python
import jax
import jax.numpy as jnp
from jax import lax
from jax.sharding import PartitionSpec as P


def from_behind(block, axis, distance):
    devices = range(lax.axis_size(axis))
    route = [(i - distance, i) for i in devices if i - distance in devices]
    return lax.ppermute(block, axis, route)


def shift_front(values, axis):
    widths = [(0, 0)] * values.ndim
    widths[axis] = (1, 0)
    return jnp.pad(lax.slice_in_dim(values, 0, values.shape[axis] - 1, 1, axis), widths)


def shift_back(values, axis):
    widths = [(0, 0)] * values.ndim
    widths[axis] = (0, 1)
    return jnp.pad(lax.slice_in_dim(values, 1, values.shape[axis], 1, axis), widths)


def transposed_phases(source, taps):
    shift_row = shift_back(source, 2)
    shift_col = shift_back(source, 4)
    shift_both = shift_back(shift_row, 4)
    sources = {(0, 0): source, (1, 0): shift_row, (0, 1): shift_col, (1, 1): shift_both}
    phases = {}
    for row_tap in range(3):
        for col_tap in range(3):
            picked = sources[int(row_tap == 0), int(col_tap == 0)]
            term = jnp.einsum(
                "bdhew,ce->bdhcw",
                picked,
                taps[row_tap, col_tap],
                preferred_element_type=jnp.float32,
            )
            place = (0 if row_tap == 1 else 1, 0 if col_tap == 1 else 1)
            phases[place] = term if place not in phases else phases[place] + term
    upper = jnp.stack([phases[0, 0], phases[0, 1]], axis=4)
    lower = jnp.stack([phases[1, 0], phases[1, 1]], axis=4)
    return jnp.stack([upper, lower], axis=3)


def chan_shift(block, shift):
    size = lax.axis_size("chan")
    return lax.ppermute(block, "chan", [(i, (i + shift) % size) for i in range(size)])


def from_next_slab(block, chan_offset):
    slabs = lax.axis_size("space")
    size = lax.axis_size("chan")
    route = [
        ((s + 1) * size + (c + chan_offset) % size, s * size + c)
        for s in range(slabs - 1)
        for c in range(size)
    ]
    return lax.ppermute(block, ("space", "chan"), route)


def per_device(volume, kernel, cotangent):
    count, planes_in, rows_in, chans_in, cols_in = volume.shape
    planes_out = planes_in // 2
    rows_out = rows_in // 2
    cols_out = cols_in // 2
    chans_out = kernel.shape[2]
    groups = lax.axis_size("chan")
    share = chans_out // groups
    me = lax.axis_index("chan")
    kernel = jnp.roll(kernel, -me * share, axis=2)
    below = from_behind(volume[:, -1:], "space", 1)
    extended = jnp.concatenate([below, volume, jnp.zeros_like(below)], axis=1)
    extended = extended.reshape(count, planes_out + 1, 2, rows_out, 2, chans_in, cols_out, 2)
    extended = jnp.moveaxis(extended, 7, 6)
    column_sets = [
        shift_front(extended[:, :, :, :, :, :, 1], 6),
        extended[:, :, :, :, :, :, 0],
        extended[:, :, :, :, :, :, 1],
    ]
    partial_sum = jnp.zeros((count, planes_out, rows_out, chans_out, cols_out), jnp.float32)
    for col_tap in range(3):
        columns = column_sets[col_tap]
        depth_sets = [columns[:, :planes_out, 0], columns[:, :planes_out, 1], columns[:, 1:, 0]]
        for depth_tap in range(3):
            slab = depth_sets[depth_tap]
            row_sets = [shift_front(slab[:, :, :, 1], 2), slab[:, :, :, 0], slab[:, :, :, 1]]
            for row_tap in range(3):
                index = 9 * depth_tap + 3 * row_tap + col_tap
                partial_sum = partial_sum + jnp.einsum(
                    "bdhcw,ce->bdhew",
                    row_sets[row_tap],
                    kernel[index],
                    preferred_element_type=jnp.float32,
                )
    total = partial_sum[:, :, :, :share]
    for k in range(1, groups):
        total = total + chan_shift(partial_sum[:, :, :, k * share:(k + 1) * share], k)
    response = total.astype(jnp.bfloat16)
    own = [cotangent] + [chan_shift(cotangent, -k) for k in range(1, groups)]
    following = [from_next_slab(cotangent, k) for k in range(groups)]
    full_cot = jnp.concatenate(own, axis=3)
    next_cot = jnp.concatenate(following, axis=3)
    taps = kernel.reshape(3, 3, 3, chans_in, chans_out)
    even_planes = transposed_phases(full_cot, taps[1])
    odd_planes = transposed_phases(next_cot, taps[0]) + transposed_phases(full_cot, taps[2])
    both = jnp.stack([even_planes, odd_planes], axis=2).astype(jnp.bfloat16)
    both = jnp.moveaxis(both, 6, 7)
    volume_grad = both.reshape(count, planes_in, rows_in, chans_in, cols_in)
    return (response, volume_grad)


def solution(mesh):
    placed = (
        P("dp", "space", None, "chan", None),
        P(None, "chan", None),
        P("dp", "space", None, "chan", None),
    )
    return jax.shard_map(
        per_device,
        mesh=mesh,
        in_specs=placed,
        out_specs=(P("dp", "space", None, "chan", None), P("dp", "space", None, "chan", None)),
        check_vma=False,
    )
```

```python
import jax
import jax.numpy as jnp
from jax import lax
from jax.sharding import PartitionSpec as P
from jax.experimental import pallas as pl
from jax.experimental.pallas import tpu as pltpu


def from_behind(block, axis, distance):
    devices = range(lax.axis_size(axis))
    route = [(i - distance, i) for i in devices if i - distance in devices]
    return lax.ppermute(block, axis, route)


def shift_front(values, axis):
    widths = [(0, 0)] * values.ndim
    widths[axis] = (1, 0)
    return jnp.pad(lax.slice_in_dim(values, 0, values.shape[axis] - 1, 1, axis), widths)


def shift_back(values, axis):
    widths = [(0, 0)] * values.ndim
    widths[axis] = (0, 1)
    return jnp.pad(lax.slice_in_dim(values, 1, values.shape[axis], 1, axis), widths)


def transposed_phases(source, taps):
    shift_row = shift_back(source, 2)
    shift_col = shift_back(source, 4)
    shift_both = shift_back(shift_row, 4)
    sources = {(0, 0): source, (1, 0): shift_row, (0, 1): shift_col, (1, 1): shift_both}
    phases = {}
    for row_tap in range(3):
        for col_tap in range(3):
            picked = sources[int(row_tap == 0), int(col_tap == 0)]
            term = jnp.einsum(
                "bdhew,ce->bdhcw",
                picked,
                taps[row_tap, col_tap],
                preferred_element_type=jnp.float32,
            )
            place = (0 if row_tap == 1 else 1, 0 if col_tap == 1 else 1)
            phases[place] = term if place not in phases else phases[place] + term
    upper = jnp.stack([phases[0, 0], phases[0, 1]], axis=4)
    lower = jnp.stack([phases[1, 0], phases[1, 1]], axis=4)
    return jnp.stack([upper, lower], axis=3)


def forward_rows(halo_ref, vol_ref, sel_ref, kbig_ref, out_ref, picked_ref):
    planes, rows, chans, cols = vol_ref.shape
    rows_out = out_ref.shape[0]
    cols_out = out_ref.shape[2]
    sel = sel_ref[...]
    for plane in range(planes + 1):
        source = halo_ref[...] if plane == 0 else vol_ref[plane - 1]
        flat = source.reshape(rows * chans, cols)
        chosen = jnp.dot(flat, sel, preferred_element_type=jnp.float32)
        picked_ref[plane] = chosen.astype(picked_ref.dtype).reshape(rows, chans, 3 * cols_out)
    kbig = kbig_ref[...]
    zero = jnp.zeros((chans, cols_out), picked_ref.dtype)
    for i in range(rows_out):
        pieces = []
        for depth_tap in range(3):
            for row_tap in range(3):
                row = 2 * i + row_tap - 1
                for col_tap in range(3):
                    if row < 0:
                        pieces.append(zero)
                    else:
                        pieces.append(picked_ref[depth_tap, row, :, col_tap * cols_out:(col_tap + 1) * cols_out])
        stacked = jnp.concatenate(pieces, axis=0)
        out_ref[i] = jnp.dot(kbig, stacked, preferred_element_type=jnp.float32)


def forward_partial(halo, vol, kernel):
    planes, rows, chans, cols = vol.shape
    taps, _, chans_out = kernel.shape
    rows_out, cols_out = rows // 2, cols // 2
    w = jnp.arange(cols)[:, None]
    k = jnp.arange(3 * cols_out)[None, :]
    sel = (w == 2 * (k % cols_out) + k // cols_out - 1).astype(vol.dtype)
    kbig = jnp.transpose(kernel, (2, 0, 1)).reshape(chans_out, taps * chans)
    flops = 2 * (planes + 1) * rows * chans * cols * 3 * cols_out + 2 * rows_out * chans_out * taps * chans * cols_out
    return pl.pallas_call(
        forward_rows,
        out_shape=jax.ShapeDtypeStruct((rows_out, chans_out, cols_out), jnp.float32),
        in_specs=[pl.BlockSpec(memory_space=pltpu.VMEM)] * 4,
        out_specs=pl.BlockSpec(memory_space=pltpu.VMEM),
        scratch_shapes=[pltpu.VMEM((planes + 1, rows, chans, 3 * cols_out), vol.dtype)],
        cost_estimate=pl.CostEstimate(flops=flops, bytes_accessed=2 * 4 * vol.size, transcendentals=0),
    )(halo, vol, sel, kbig)


def chan_shift(block, shift):
    size = lax.axis_size("chan")
    return lax.ppermute(block, "chan", [(i, (i + shift) % size) for i in range(size)])


def from_next_slab(block, chan_offset):
    slabs = lax.axis_size("space")
    size = lax.axis_size("chan")
    route = [
        ((s + 1) * size + (c + chan_offset) % size, s * size + c)
        for s in range(slabs - 1)
        for c in range(size)
    ]
    return lax.ppermute(block, ("space", "chan"), route)


def per_device(volume, kernel, cotangent):
    count, planes_in, rows_in, chans_in, cols_in = volume.shape
    planes_out = planes_in // 2
    rows_out = rows_in // 2
    cols_out = cols_in // 2
    chans_out = kernel.shape[2]
    groups = lax.axis_size("chan")
    share = chans_out // groups
    me = lax.axis_index("chan")
    kernel = jnp.roll(kernel, -me * share, axis=2)
    below = from_behind(volume[:, -1:], "space", 1)
    partial_sum = forward_partial(below[0, 0], volume[0], kernel)
    partial_sum = partial_sum.reshape(count, planes_out, rows_out, chans_out, cols_out)
    total = partial_sum[:, :, :, :share]
    for k in range(1, groups):
        total = total + chan_shift(partial_sum[:, :, :, k * share:(k + 1) * share], k)
    response = total.astype(jnp.bfloat16)
    own = [cotangent] + [chan_shift(cotangent, -k) for k in range(1, groups)]
    following = [from_next_slab(cotangent, k) for k in range(groups)]
    full_cot = jnp.concatenate(own, axis=3)
    next_cot = jnp.concatenate(following, axis=3)
    taps = kernel.reshape(3, 3, 3, chans_in, chans_out)
    even_planes = transposed_phases(full_cot, taps[1])
    odd_planes = transposed_phases(next_cot, taps[0]) + transposed_phases(full_cot, taps[2])
    both = jnp.stack([even_planes, odd_planes], axis=2).astype(jnp.bfloat16)
    both = jnp.moveaxis(both, 6, 7)
    volume_grad = both.reshape(count, planes_in, rows_in, chans_in, cols_in)
    return (response, volume_grad)


def solution(mesh):
    placed = (
        P("dp", "space", None, "chan", None),
        P(None, "chan", None),
        P("dp", "space", None, "chan", None),
    )
    return jax.shard_map(
        per_device,
        mesh=mesh,
        in_specs=placed,
        out_specs=(P("dp", "space", None, "chan", None), P("dp", "space", None, "chan", None)),
        check_vma=False,
    )
```

```python
import jax
import jax.numpy as jnp
from jax import lax
from jax.sharding import PartitionSpec as P
from jax.experimental import pallas as pl
from jax.experimental.pallas import tpu as pltpu


def from_behind(block, axis, distance):
    devices = range(lax.axis_size(axis))
    route = [(i - distance, i) for i in devices if i - distance in devices]
    return lax.ppermute(block, axis, route)


def shift_front(values, axis):
    widths = [(0, 0)] * values.ndim
    widths[axis] = (1, 0)
    return jnp.pad(lax.slice_in_dim(values, 0, values.shape[axis] - 1, 1, axis), widths)


def shift_back(values, axis):
    widths = [(0, 0)] * values.ndim
    widths[axis] = (0, 1)
    return jnp.pad(lax.slice_in_dim(values, 1, values.shape[axis], 1, axis), widths)


def transposed_phases(source, taps):
    shift_row = shift_back(source, 2)
    shift_col = shift_back(source, 4)
    shift_both = shift_back(shift_row, 4)
    sources = {(0, 0): source, (1, 0): shift_row, (0, 1): shift_col, (1, 1): shift_both}
    phases = {}
    for row_tap in range(3):
        for col_tap in range(3):
            picked = sources[int(row_tap == 0), int(col_tap == 0)]
            term = jnp.einsum(
                "bdhew,ce->bdhcw",
                picked,
                taps[row_tap, col_tap],
                preferred_element_type=jnp.float32,
            )
            place = (0 if row_tap == 1 else 1, 0 if col_tap == 1 else 1)
            phases[place] = term if place not in phases else phases[place] + term
    upper = jnp.stack([phases[0, 0], phases[0, 1]], axis=4)
    lower = jnp.stack([phases[1, 0], phases[1, 1]], axis=4)
    return jnp.stack([upper, lower], axis=3)


def forward_rows(halo_ref, vol_ref, sel_ref, kbig_ref, out_ref, picked_ref):
    planes, rows, chans, cols = vol_ref.shape
    rows_out = out_ref.shape[0]
    cols_out = out_ref.shape[2]
    sel = sel_ref[...]
    for plane in range(planes + 1):
        source = halo_ref[...] if plane == 0 else vol_ref[plane - 1]
        flat = source.reshape(rows * chans, cols)
        chosen = jnp.dot(flat, sel, preferred_element_type=jnp.float32)
        picked_ref[plane] = chosen.astype(picked_ref.dtype).reshape(rows, chans, 3 * cols_out)
    kbig = kbig_ref[...]
    zero = jnp.zeros((chans, cols_out), picked_ref.dtype)
    for i in range(rows_out):
        pieces = []
        for depth_tap in range(3):
            for row_tap in range(3):
                row = 2 * i + row_tap - 1
                for col_tap in range(3):
                    if row < 0:
                        pieces.append(zero)
                    else:
                        pieces.append(picked_ref[depth_tap, row, :, col_tap * cols_out:(col_tap + 1) * cols_out])
        stacked = jnp.concatenate(pieces, axis=0)
        out_ref[i] = jnp.dot(kbig, stacked, preferred_element_type=jnp.float32)


def forward_partial(halo, vol, kernel):
    planes, rows, chans, cols = vol.shape
    taps, _, chans_out = kernel.shape
    rows_out, cols_out = rows // 2, cols // 2
    w = jnp.arange(cols)[:, None]
    k = jnp.arange(3 * cols_out)[None, :]
    sel = (w == 2 * (k % cols_out) + k // cols_out - 1).astype(vol.dtype)
    kbig = jnp.transpose(kernel, (2, 0, 1)).reshape(chans_out, taps * chans)
    flops = 2 * (planes + 1) * rows * chans * cols * 3 * cols_out + 2 * rows_out * chans_out * taps * chans * cols_out
    return pl.pallas_call(
        forward_rows,
        out_shape=jax.ShapeDtypeStruct((rows_out, chans_out, cols_out), jnp.float32),
        in_specs=[pl.BlockSpec(memory_space=pltpu.VMEM)] * 4,
        out_specs=pl.BlockSpec(memory_space=pltpu.VMEM),
        scratch_shapes=[pltpu.VMEM((planes + 1, rows, chans, 3 * cols_out), vol.dtype)],
        cost_estimate=pl.CostEstimate(flops=flops, bytes_accessed=2 * 4 * vol.size, transcendentals=0),
    )(halo, vol, sel, kbig)


def chan_shift(block, shift):
    size = lax.axis_size("chan")
    return lax.ppermute(block, "chan", [(i, (i + shift) % size) for i in range(size)])


def per_device(volume, kernel, cotangent):
    count, planes_in, rows_in, chans_in, cols_in = volume.shape
    planes_out = planes_in // 2
    rows_out = rows_in // 2
    cols_out = cols_in // 2
    chans_out = kernel.shape[2]
    groups = lax.axis_size("chan")
    share = chans_out // groups
    me = lax.axis_index("chan")
    kernel = jnp.roll(kernel, -me * share, axis=2)
    below = from_behind(volume[:, -1:], "space", 1)
    partial_sum = forward_partial(below[0, 0], volume[0], kernel)
    partial_sum = partial_sum.reshape(count, planes_out, rows_out, chans_out, cols_out)
    total = partial_sum[:, :, :, :share]
    for k in range(1, groups):
        total = total + chan_shift(partial_sum[:, :, :, k * share:(k + 1) * share], k)
    response = total.astype(jnp.bfloat16)
    pair = jnp.concatenate([cotangent, from_behind(cotangent, "space", -1)], axis=1)
    pieces = [pair] + [chan_shift(pair, -k) for k in range(1, groups)]
    both_cot = jnp.concatenate(pieces, axis=3)
    full_cot = both_cot[:, :1]
    next_cot = both_cot[:, 1:]
    taps = kernel.reshape(3, 3, 3, chans_in, chans_out)
    even_planes = transposed_phases(full_cot, taps[1])
    odd_planes = transposed_phases(next_cot, taps[0]) + transposed_phases(full_cot, taps[2])
    both = jnp.stack([even_planes, odd_planes], axis=2).astype(jnp.bfloat16)
    both = jnp.moveaxis(both, 6, 7)
    volume_grad = both.reshape(count, planes_in, rows_in, chans_in, cols_in)
    return (response, volume_grad)


def solution(mesh):
    placed = (
        P("dp", "space", None, "chan", None),
        P(None, "chan", None),
        P("dp", "space", None, "chan", None),
    )
    return jax.shard_map(
        per_device,
        mesh=mesh,
        in_specs=placed,
        out_specs=(P("dp", "space", None, "chan", None), P("dp", "space", None, "chan", None)),
        check_vma=False,
    )
```

```python
import jax
import jax.numpy as jnp
from jax import lax
from jax.sharding import PartitionSpec as P
from jax.experimental import pallas as pl
from jax.experimental.pallas import tpu as pltpu


def from_behind(block, axis, distance):
    devices = range(lax.axis_size(axis))
    route = [(i - distance, i) for i in devices if i - distance in devices]
    return lax.ppermute(block, axis, route)


def shift_front(values, axis):
    widths = [(0, 0)] * values.ndim
    widths[axis] = (1, 0)
    return jnp.pad(lax.slice_in_dim(values, 0, values.shape[axis] - 1, 1, axis), widths)


def shift_back(values, axis):
    widths = [(0, 0)] * values.ndim
    widths[axis] = (0, 1)
    return jnp.pad(lax.slice_in_dim(values, 1, values.shape[axis], 1, axis), widths)


def transposed_phases(source, taps):
    shift_row = shift_back(source, 2)
    shift_col = shift_back(source, 4)
    shift_both = shift_back(shift_row, 4)
    sources = {(0, 0): source, (1, 0): shift_row, (0, 1): shift_col, (1, 1): shift_both}
    phases = {}
    for row_tap in range(3):
        for col_tap in range(3):
            picked = sources[int(row_tap == 0), int(col_tap == 0)]
            term = jnp.einsum(
                "bdhew,ce->bdhcw",
                picked,
                taps[row_tap, col_tap],
                preferred_element_type=jnp.float32,
            )
            place = (0 if row_tap == 1 else 1, 0 if col_tap == 1 else 1)
            phases[place] = term if place not in phases else phases[place] + term
    upper = jnp.stack([phases[0, 0], phases[0, 1]], axis=4)
    lower = jnp.stack([phases[1, 0], phases[1, 1]], axis=4)
    return jnp.stack([upper, lower], axis=3)


def forward_rows(halo_ref, vol_ref, sel_ref, kbig_ref, out_ref, picked_ref):
    planes, rows, chans, cols = vol_ref.shape
    rows_out = out_ref.shape[0]
    cols_out = out_ref.shape[2]
    sel = sel_ref[...]
    for plane in range(planes + 1):
        source = halo_ref[...] if plane == 0 else vol_ref[plane - 1]
        flat = source.reshape(rows * chans, cols)
        chosen = jnp.dot(flat, sel, preferred_element_type=jnp.float32)
        picked_ref[plane] = chosen.astype(picked_ref.dtype).reshape(rows, chans, 3 * cols_out)
    kbig = kbig_ref[...]
    zero = jnp.zeros((chans, cols_out), picked_ref.dtype)
    for i in range(rows_out):
        pieces = []
        for depth_tap in range(3):
            for row_tap in range(3):
                row = 2 * i + row_tap - 1
                for col_tap in range(3):
                    if row < 0:
                        pieces.append(zero)
                    else:
                        pieces.append(picked_ref[depth_tap, row, :, col_tap * cols_out:(col_tap + 1) * cols_out])
        stacked = jnp.concatenate(pieces, axis=0)
        out_ref[i] = jnp.dot(kbig, stacked, preferred_element_type=jnp.float32)


def forward_partial(halo, vol, kernel):
    planes, rows, chans, cols = vol.shape
    taps, _, chans_out = kernel.shape
    rows_out, cols_out = rows // 2, cols // 2
    w = jnp.arange(cols)[:, None]
    k = jnp.arange(3 * cols_out)[None, :]
    sel = (w == 2 * (k % cols_out) + k // cols_out - 1).astype(vol.dtype)
    kbig = jnp.transpose(kernel, (2, 0, 1)).reshape(chans_out, taps * chans)
    flops = 2 * (planes + 1) * rows * chans * cols * 3 * cols_out + 2 * rows_out * chans_out * taps * chans * cols_out
    return pl.pallas_call(
        forward_rows,
        out_shape=jax.ShapeDtypeStruct((rows_out, chans_out, cols_out), jnp.float32),
        in_specs=[pl.BlockSpec(memory_space=pltpu.VMEM)] * 4,
        out_specs=pl.BlockSpec(memory_space=pltpu.VMEM),
        scratch_shapes=[pltpu.VMEM((planes + 1, rows, chans, 3 * cols_out), vol.dtype)],
        cost_estimate=pl.CostEstimate(flops=flops, bytes_accessed=2 * 4 * vol.size, transcendentals=0),
    )(halo, vol, sel, kbig)


def chan_shift(block, shift):
    size = lax.axis_size("chan")
    return lax.ppermute(block, "chan", [(i, (i + shift) % size) for i in range(size)])


def per_device(volume, kernel, cotangent):
    count, planes_in, rows_in, chans_in, cols_in = volume.shape
    planes_out = planes_in // 2
    rows_out = rows_in // 2
    cols_out = cols_in // 2
    chans_out = kernel.shape[2]
    groups = lax.axis_size("chan")
    share = chans_out // groups
    me = lax.axis_index("chan")
    kernel = jnp.roll(kernel, -me * share, axis=2)
    below = from_behind(volume[:, -1:], "space", 1)
    partial_sum = forward_partial(below[0, 0], volume[0], kernel)
    partial_sum = partial_sum.reshape(count, planes_out, rows_out, chans_out, cols_out)
    pair = jnp.concatenate([cotangent, from_behind(cotangent, "space", -1)], axis=1)
    partial_sum, pair = lax.optimization_barrier((partial_sum, pair))
    total = partial_sum[:, :, :, :share]
    for k in range(1, groups):
        total = total + chan_shift(partial_sum[:, :, :, k * share:(k + 1) * share], k)
    response = total.astype(jnp.bfloat16)
    pieces = [pair] + [chan_shift(pair, -k) for k in range(1, groups)]
    both_cot = jnp.concatenate(pieces, axis=3)
    full_cot = both_cot[:, :1]
    next_cot = both_cot[:, 1:]
    taps = kernel.reshape(3, 3, 3, chans_in, chans_out)
    even_planes = transposed_phases(full_cot, taps[1])
    odd_planes = transposed_phases(next_cot, taps[0]) + transposed_phases(full_cot, taps[2])
    both = jnp.stack([even_planes, odd_planes], axis=2).astype(jnp.bfloat16)
    both = jnp.moveaxis(both, 6, 7)
    volume_grad = both.reshape(count, planes_in, rows_in, chans_in, cols_in)
    return (response, volume_grad)


def solution(mesh):
    placed = (
        P("dp", "space", None, "chan", None),
        P(None, "chan", None),
        P("dp", "space", None, "chan", None),
    )
    return jax.shard_map(
        per_device,
        mesh=mesh,
        in_specs=placed,
        out_specs=(P("dp", "space", None, "chan", None), P("dp", "space", None, "chan", None)),
        check_vma=False,
    )
```

```python
import jax
import jax.numpy as jnp
from jax import lax
from jax.sharding import PartitionSpec as P
from jax.experimental import pallas as pl
from jax.experimental.pallas import tpu as pltpu


def from_behind(block, axis, distance):
    devices = range(lax.axis_size(axis))
    route = [(i - distance, i) for i in devices if i - distance in devices]
    return lax.ppermute(block, axis, route)


def shift_front(values, axis):
    widths = [(0, 0)] * values.ndim
    widths[axis] = (1, 0)
    return jnp.pad(lax.slice_in_dim(values, 0, values.shape[axis] - 1, 1, axis), widths)


def shift_back(values, axis):
    widths = [(0, 0)] * values.ndim
    widths[axis] = (0, 1)
    return jnp.pad(lax.slice_in_dim(values, 1, values.shape[axis], 1, axis), widths)


def transposed_phases(source, taps):
    shift_row = shift_back(source, 2)
    shift_col = shift_back(source, 4)
    shift_both = shift_back(shift_row, 4)
    sources = {(0, 0): source, (1, 0): shift_row, (0, 1): shift_col, (1, 1): shift_both}
    phases = {}
    for row_tap in range(3):
        for col_tap in range(3):
            picked = sources[int(row_tap == 0), int(col_tap == 0)]
            term = jnp.einsum(
                "bdhew,ce->bdhcw",
                picked,
                taps[row_tap, col_tap],
                preferred_element_type=jnp.float32,
            )
            place = (0 if row_tap == 1 else 1, 0 if col_tap == 1 else 1)
            phases[place] = term if place not in phases else phases[place] + term
    upper = jnp.stack([phases[0, 0], phases[0, 1]], axis=4)
    lower = jnp.stack([phases[1, 0], phases[1, 1]], axis=4)
    return jnp.stack([upper, lower], axis=3)


def forward_rows(halo_ref, vol_ref, sel_ref, kbig_ref, out_ref, picked_ref):
    planes, rows, chans, cols = vol_ref.shape
    rows_out = out_ref.shape[0]
    cols_out = out_ref.shape[2]
    sel = sel_ref[...]
    for plane in range(planes + 1):
        source = halo_ref[...] if plane == 0 else vol_ref[plane - 1]
        flat = source.reshape(rows * chans, cols)
        chosen = jnp.dot(flat, sel, preferred_element_type=jnp.float32)
        picked_ref[plane] = chosen.astype(picked_ref.dtype).reshape(rows, chans, 3 * cols_out)
    kbig = kbig_ref[...]
    zero = jnp.zeros((chans, cols_out), picked_ref.dtype)
    for i in range(rows_out):
        pieces = []
        for depth_tap in range(3):
            for row_tap in range(3):
                row = 2 * i + row_tap - 1
                for col_tap in range(3):
                    if row < 0:
                        pieces.append(zero)
                    else:
                        pieces.append(picked_ref[depth_tap, row, :, col_tap * cols_out:(col_tap + 1) * cols_out])
        stacked = jnp.concatenate(pieces, axis=0)
        out_ref[i] = jnp.dot(kbig, stacked, preferred_element_type=jnp.float32)


def forward_partial(halo, vol, kernel):
    planes, rows, chans, cols = vol.shape
    taps, _, chans_out = kernel.shape
    rows_out, cols_out = rows // 2, cols // 2
    w = jnp.arange(cols)[:, None]
    k = jnp.arange(3 * cols_out)[None, :]
    sel = (w == 2 * (k % cols_out) + k // cols_out - 1).astype(vol.dtype)
    kbig = jnp.transpose(kernel, (2, 0, 1)).reshape(chans_out, taps * chans)
    flops = 2 * (planes + 1) * rows * chans * cols * 3 * cols_out + 2 * rows_out * chans_out * taps * chans * cols_out
    return pl.pallas_call(
        forward_rows,
        out_shape=jax.ShapeDtypeStruct((rows_out, chans_out, cols_out), jnp.float32),
        in_specs=[pl.BlockSpec(memory_space=pltpu.VMEM)] * 4,
        out_specs=pl.BlockSpec(memory_space=pltpu.VMEM),
        scratch_shapes=[pltpu.VMEM((planes + 1, rows, chans, 3 * cols_out), vol.dtype)],
        cost_estimate=pl.CostEstimate(flops=flops, bytes_accessed=2 * 4 * vol.size, transcendentals=0),
    )(halo, vol, sel, kbig)


def backward_rows(cot_ref, k_ref, tsel_ref, out_ref, up_ref):
    planes, rows_out, chans_out, cols_out = cot_ref.shape
    rows = out_ref.shape[1]
    cols = out_ref.shape[3]
    tsel = tsel_ref[...]
    for plane in range(planes):
        flat = cot_ref[plane].reshape(rows_out * chans_out, cols_out)
        spread = jnp.dot(flat, tsel, preferred_element_type=jnp.float32)
        up_ref[plane] = spread.astype(up_ref.dtype).reshape(rows_out, chans_out, 3 * cols)
    for depth in range(2):
        sources = [(1, 0)] if depth == 0 else [(2, 0), (0, 1)]
        for row in range(rows):
            weights, values = [], []
            for depth_tap, plane in sources:
                for row_tap in range(3):
                    if (row + 1 - row_tap) % 2:
                        continue
                    i = (row + 1 - row_tap) // 2
                    if not 0 <= i < rows_out:
                        continue
                    for col_tap in range(3):
                        weights.append(k_ref[9 * depth_tap + 3 * row_tap + col_tap])
                        values.append(up_ref[plane, i, :, col_tap * cols:(col_tap + 1) * cols])
            lhs = jnp.concatenate(weights, axis=1)
            rhs = jnp.concatenate(values, axis=0)
            out_ref[depth, row] = jnp.dot(lhs, rhs, preferred_element_type=jnp.float32).astype(out_ref.dtype)


def backward_grad(cot, kernel):
    planes, rows_out, chans_out, cols_out = cot.shape
    taps, chans, _ = kernel.shape
    rows, cols = 2 * rows_out, 2 * cols_out
    j = jnp.arange(cols_out)[:, None]
    k = jnp.arange(3 * cols)[None, :]
    tsel = (k % cols == 2 * j + k // cols - 1).astype(cot.dtype)
    flops = 2 * planes * rows_out * chans_out * cols_out * 3 * cols + 2 * 2 * rows * chans * 9 * chans_out * cols
    return pl.pallas_call(
        backward_rows,
        out_shape=jax.ShapeDtypeStruct((2, rows, chans, cols), cot.dtype),
        in_specs=[pl.BlockSpec(memory_space=pltpu.VMEM)] * 3,
        out_specs=pl.BlockSpec(memory_space=pltpu.VMEM),
        scratch_shapes=[pltpu.VMEM((planes, rows_out, chans_out, 3 * cols), cot.dtype)],
        cost_estimate=pl.CostEstimate(flops=flops, bytes_accessed=2 * cot.size + 2 * 2 * rows * chans * cols, transcendentals=0),
    )(cot, kernel, tsel)


def chan_shift(block, shift):
    size = lax.axis_size("chan")
    return lax.ppermute(block, "chan", [(i, (i + shift) % size) for i in range(size)])


def per_device(volume, kernel, cotangent):
    count, planes_in, rows_in, chans_in, cols_in = volume.shape
    planes_out = planes_in // 2
    rows_out = rows_in // 2
    cols_out = cols_in // 2
    chans_out = kernel.shape[2]
    groups = lax.axis_size("chan")
    share = chans_out // groups
    me = lax.axis_index("chan")
    kernel = jnp.roll(kernel, -me * share, axis=2)
    below = from_behind(volume[:, -1:], "space", 1)
    partial_sum = forward_partial(below[0, 0], volume[0], kernel)
    partial_sum = partial_sum.reshape(count, planes_out, rows_out, chans_out, cols_out)
    pair = jnp.concatenate([cotangent, from_behind(cotangent, "space", -1)], axis=1)
    partial_sum, pair = lax.optimization_barrier((partial_sum, pair))
    total = partial_sum[:, :, :, :share]
    for k in range(1, groups):
        total = total + chan_shift(partial_sum[:, :, :, k * share:(k + 1) * share], k)
    response = total.astype(jnp.bfloat16)
    pieces = [pair] + [chan_shift(pair, -k) for k in range(1, groups)]
    both_cot = jnp.concatenate(pieces, axis=3)
    volume_grad = backward_grad(both_cot[0], kernel).reshape(count, planes_in, rows_in, chans_in, cols_in)
    return (response, volume_grad)


def solution(mesh):
    placed = (
        P("dp", "space", None, "chan", None),
        P(None, "chan", None),
        P("dp", "space", None, "chan", None),
    )
    return jax.shard_map(
        per_device,
        mesh=mesh,
        in_specs=placed,
        out_specs=(P("dp", "space", None, "chan", None), P("dp", "space", None, "chan", None)),
        check_vma=False,
    )
```

```python
import jax
import jax.numpy as jnp
from jax import lax
from jax.sharding import PartitionSpec as P
from jax.experimental import pallas as pl
from jax.experimental.pallas import tpu as pltpu


def from_behind(block, axis, distance):
    devices = range(lax.axis_size(axis))
    route = [(i - distance, i) for i in devices if i - distance in devices]
    return lax.ppermute(block, axis, route)


def shift_front(values, axis):
    widths = [(0, 0)] * values.ndim
    widths[axis] = (1, 0)
    return jnp.pad(lax.slice_in_dim(values, 0, values.shape[axis] - 1, 1, axis), widths)


def shift_back(values, axis):
    widths = [(0, 0)] * values.ndim
    widths[axis] = (0, 1)
    return jnp.pad(lax.slice_in_dim(values, 1, values.shape[axis], 1, axis), widths)


def transposed_phases(source, taps):
    shift_row = shift_back(source, 2)
    shift_col = shift_back(source, 4)
    shift_both = shift_back(shift_row, 4)
    sources = {(0, 0): source, (1, 0): shift_row, (0, 1): shift_col, (1, 1): shift_both}
    phases = {}
    for row_tap in range(3):
        for col_tap in range(3):
            picked = sources[int(row_tap == 0), int(col_tap == 0)]
            term = jnp.einsum(
                "bdhew,ce->bdhcw",
                picked,
                taps[row_tap, col_tap],
                preferred_element_type=jnp.float32,
            )
            place = (0 if row_tap == 1 else 1, 0 if col_tap == 1 else 1)
            phases[place] = term if place not in phases else phases[place] + term
    upper = jnp.stack([phases[0, 0], phases[0, 1]], axis=4)
    lower = jnp.stack([phases[1, 0], phases[1, 1]], axis=4)
    return jnp.stack([upper, lower], axis=3)


def spread_matrix(rows, cols, transposed):
    blocks = []
    for tap in range(3):
        narrow = lax.broadcasted_iota(jnp.int32, (rows, cols), 1 if not transposed else 0)
        wide = lax.broadcasted_iota(jnp.int32, (rows, cols), 0 if not transposed else 1)
        blocks.append(jnp.where(wide == 2 * narrow + tap - 1, 1.0, 0.0).astype(jnp.bfloat16))
    return jnp.concatenate(blocks, axis=1)


def forward_rows(halo_ref, vol_ref, kbig_ref, *refs):
    out_refs, picked_ref = refs[:-1], refs[-1]
    planes, rows, chans, cols = vol_ref.shape
    rows_out, share, cols_out = out_refs[0].shape
    sel = spread_matrix(cols, cols_out, False)
    for plane in range(planes + 1):
        source = halo_ref[...] if plane == 0 else vol_ref[plane - 1]
        flat = source.reshape(rows * chans, cols)
        chosen = jnp.dot(flat, sel, preferred_element_type=jnp.float32)
        picked_ref[plane] = chosen.astype(picked_ref.dtype).reshape(rows, chans, 3 * cols_out)
    kbig = kbig_ref[...]
    zero = jnp.zeros((chans, cols_out), picked_ref.dtype)
    for i in range(rows_out):
        pieces = []
        for depth_tap in range(3):
            for row_tap in range(3):
                row = 2 * i + row_tap - 1
                for col_tap in range(3):
                    if row < 0:
                        pieces.append(zero)
                    else:
                        pieces.append(picked_ref[depth_tap, row, :, col_tap * cols_out:(col_tap + 1) * cols_out])
        stacked = jnp.concatenate(pieces, axis=0)
        result = jnp.dot(kbig, stacked, preferred_element_type=jnp.float32)
        for k, out_ref in enumerate(out_refs):
            out_ref[i] = result[k * share:(k + 1) * share]


def forward_partial(halo, vol, kernel, groups):
    planes, rows, chans, cols = vol.shape
    taps, _, chans_out = kernel.shape
    rows_out, cols_out = rows // 2, cols // 2
    share = chans_out // groups
    kbig = jnp.transpose(kernel, (2, 0, 1)).reshape(chans_out, taps * chans)
    flops = 2 * (planes + 1) * rows * chans * cols * 3 * cols_out + 2 * rows_out * chans_out * taps * chans * cols_out
    return pl.pallas_call(
        forward_rows,
        out_shape=[jax.ShapeDtypeStruct((rows_out, share, cols_out), jnp.float32)] * groups,
        in_specs=[pl.BlockSpec(memory_space=pltpu.VMEM)] * 3,
        out_specs=[pl.BlockSpec(memory_space=pltpu.VMEM)] * groups,
        scratch_shapes=[pltpu.VMEM((planes + 1, rows, chans, 3 * cols_out), vol.dtype)],
        cost_estimate=pl.CostEstimate(flops=flops, bytes_accessed=2 * 4 * vol.size, transcendentals=0),
    )(halo, vol, kbig)


def backward_rows(*refs):
    groups = (len(refs) - 3)
    cot_refs, k_ref, out_ref, up_ref = refs[:groups], refs[groups], refs[groups + 1], refs[groups + 2]
    planes, rows_out, share, cols_out = cot_refs[0].shape
    rows = out_ref.shape[1]
    cols = out_ref.shape[3]
    tsel = spread_matrix(cols_out, cols, True)
    for k, cot_ref in enumerate(cot_refs):
        flat = cot_ref[...].reshape(planes * rows_out * share, cols_out)
        spread = jnp.dot(flat, tsel, preferred_element_type=jnp.float32)
        up_ref[:, :, k * share:(k + 1) * share, :] = spread.astype(up_ref.dtype).reshape(planes, rows_out, share, 3 * cols)
    for depth in range(2):
        sources = [(1, 0)] if depth == 0 else [(2, 0), (0, 1)]
        for row in range(rows):
            weights, values = [], []
            for depth_tap, plane in sources:
                for row_tap in range(3):
                    if (row + 1 - row_tap) % 2:
                        continue
                    i = (row + 1 - row_tap) // 2
                    if not 0 <= i < rows_out:
                        continue
                    for col_tap in range(3):
                        weights.append(k_ref[9 * depth_tap + 3 * row_tap + col_tap])
                        values.append(up_ref[plane, i, :, col_tap * cols:(col_tap + 1) * cols])
            lhs = jnp.concatenate(weights, axis=1)
            rhs = jnp.concatenate(values, axis=0)
            out_ref[depth, row] = jnp.dot(lhs, rhs, preferred_element_type=jnp.float32).astype(out_ref.dtype)


def backward_grad(pieces, kernel):
    planes, rows_out, share, cols_out = pieces[0].shape
    chans_out = share * len(pieces)
    taps, chans, _ = kernel.shape
    rows, cols = 2 * rows_out, 2 * cols_out
    flops = 2 * planes * rows_out * chans_out * cols_out * 3 * cols + 2 * 2 * rows * chans * 9 * chans_out * cols
    return pl.pallas_call(
        backward_rows,
        out_shape=jax.ShapeDtypeStruct((2, rows, chans, cols), kernel.dtype),
        in_specs=[pl.BlockSpec(memory_space=pltpu.VMEM)] * (len(pieces) + 1),
        out_specs=pl.BlockSpec(memory_space=pltpu.VMEM),
        scratch_shapes=[pltpu.VMEM((planes, rows_out, chans_out, 3 * cols), kernel.dtype)],
        cost_estimate=pl.CostEstimate(flops=flops, bytes_accessed=2 * planes * rows_out * chans_out * cols_out + 2 * 2 * rows * chans * cols, transcendentals=0),
    )(*pieces, kernel)


def chan_shift(block, shift):
    size = lax.axis_size("chan")
    return lax.ppermute(block, "chan", [(i, (i + shift) % size) for i in range(size)])


def per_device(volume, kernel, cotangent):
    count, planes_in, rows_in, chans_in, cols_in = volume.shape
    planes_out = planes_in // 2
    rows_out = rows_in // 2
    cols_out = cols_in // 2
    chans_out = kernel.shape[2]
    groups = lax.axis_size("chan")
    share = chans_out // groups
    me = lax.axis_index("chan")
    kernel = jnp.roll(kernel, -me * share, axis=2)
    below = from_behind(volume[:, -1:], "space", 1)
    chunks = forward_partial(below[0, 0], volume[0], kernel, groups)
    pair = jnp.concatenate([cotangent, from_behind(cotangent, "space", -1)], axis=1)
    chunks, pair = lax.optimization_barrier((chunks, pair))
    total = chunks[0]
    for k in range(1, groups):
        total = total + chan_shift(chunks[k], k)
    response = total.astype(jnp.bfloat16).reshape(count, planes_out, rows_out, share, cols_out)
    pieces = [pair[0]] + [chan_shift(pair[0], -k) for k in range(1, groups)]
    volume_grad = backward_grad(pieces, kernel).reshape(count, planes_in, rows_in, chans_in, cols_in)
    return (response, volume_grad)


def solution(mesh):
    placed = (
        P("dp", "space", None, "chan", None),
        P(None, "chan", None),
        P("dp", "space", None, "chan", None),
    )
    return jax.shard_map(
        per_device,
        mesh=mesh,
        in_specs=placed,
        out_specs=(P("dp", "space", None, "chan", None), P("dp", "space", None, "chan", None)),
        check_vma=False,
    )
```

```python
import jax
import jax.numpy as jnp
from jax import lax
from jax.sharding import PartitionSpec as P
from jax.experimental import pallas as pl
from jax.experimental.pallas import tpu as pltpu


def from_behind(block, axis, distance):
    devices = range(lax.axis_size(axis))
    route = [(i - distance, i) for i in devices if i - distance in devices]
    return lax.ppermute(block, axis, route)


def shift_front(values, axis):
    widths = [(0, 0)] * values.ndim
    widths[axis] = (1, 0)
    return jnp.pad(lax.slice_in_dim(values, 0, values.shape[axis] - 1, 1, axis), widths)


def shift_back(values, axis):
    widths = [(0, 0)] * values.ndim
    widths[axis] = (0, 1)
    return jnp.pad(lax.slice_in_dim(values, 1, values.shape[axis], 1, axis), widths)


def transposed_phases(source, taps):
    shift_row = shift_back(source, 2)
    shift_col = shift_back(source, 4)
    shift_both = shift_back(shift_row, 4)
    sources = {(0, 0): source, (1, 0): shift_row, (0, 1): shift_col, (1, 1): shift_both}
    phases = {}
    for row_tap in range(3):
        for col_tap in range(3):
            picked = sources[int(row_tap == 0), int(col_tap == 0)]
            term = jnp.einsum(
                "bdhew,ce->bdhcw",
                picked,
                taps[row_tap, col_tap],
                preferred_element_type=jnp.float32,
            )
            place = (0 if row_tap == 1 else 1, 0 if col_tap == 1 else 1)
            phases[place] = term if place not in phases else phases[place] + term
    upper = jnp.stack([phases[0, 0], phases[0, 1]], axis=4)
    lower = jnp.stack([phases[1, 0], phases[1, 1]], axis=4)
    return jnp.stack([upper, lower], axis=3)


def spread_matrix(rows, cols, transposed):
    blocks = []
    for tap in range(3):
        narrow = lax.broadcasted_iota(jnp.int32, (rows, cols), 1 if not transposed else 0)
        wide = lax.broadcasted_iota(jnp.int32, (rows, cols), 0 if not transposed else 1)
        blocks.append(jnp.where(wide == 2 * narrow + tap - 1, 1.0, 0.0).astype(jnp.bfloat16))
    return jnp.concatenate(blocks, axis=1)


def forward_rows(halo_ref, vol_ref, kbig_ref, pair_ref, own_ref, *refs):
    sent_refs, picked_ref = refs[:-1], refs[-1]
    planes, rows, chans, cols = vol_ref.shape
    rows_out, share, cols_out = own_ref.shape
    carried = pair_ref[...].astype(jnp.float32)
    for sent_ref in sent_refs:
        sent_ref[1:] = carried
    sel = spread_matrix(cols, cols_out, False)
    for plane in range(planes + 1):
        source = halo_ref[...] if plane == 0 else vol_ref[plane - 1]
        flat = source.reshape(rows * chans, cols)
        chosen = jnp.dot(flat, sel, preferred_element_type=jnp.float32)
        picked_ref[plane] = chosen.astype(picked_ref.dtype).reshape(rows, chans, 3 * cols_out)
    kbig = kbig_ref[...]
    zero = jnp.zeros((chans, cols_out), picked_ref.dtype)
    for i in range(rows_out):
        pieces = []
        for depth_tap in range(3):
            for row_tap in range(3):
                row = 2 * i + row_tap - 1
                for col_tap in range(3):
                    if row < 0:
                        pieces.append(zero)
                    else:
                        pieces.append(picked_ref[depth_tap, row, :, col_tap * cols_out:(col_tap + 1) * cols_out])
        stacked = jnp.concatenate(pieces, axis=0)
        result = jnp.dot(kbig, stacked, preferred_element_type=jnp.float32)
        own_ref[i] = result[:share]
        for k, sent_ref in enumerate(sent_refs, start=1):
            sent_ref[0, i] = result[k * share:(k + 1) * share]


def forward_partial(halo, vol, kernel, pair, groups):
    planes, rows, chans, cols = vol.shape
    taps, _, chans_out = kernel.shape
    rows_out, cols_out = rows // 2, cols // 2
    share = chans_out // groups
    kbig = jnp.transpose(kernel, (2, 0, 1)).reshape(chans_out, taps * chans)
    flops = 2 * (planes + 1) * rows * chans * cols * 3 * cols_out + 2 * rows_out * chans_out * taps * chans * cols_out
    sent = jax.ShapeDtypeStruct((1 + pair.shape[0], rows_out, share, cols_out), jnp.float32)
    return pl.pallas_call(
        forward_rows,
        out_shape=[jax.ShapeDtypeStruct((rows_out, share, cols_out), jnp.float32)] + [sent] * (groups - 1),
        in_specs=[pl.BlockSpec(memory_space=pltpu.VMEM)] * 4,
        out_specs=[pl.BlockSpec(memory_space=pltpu.VMEM)] * groups,
        scratch_shapes=[pltpu.VMEM((planes + 1, rows, chans, 3 * cols_out), vol.dtype)],
        cost_estimate=pl.CostEstimate(flops=flops, bytes_accessed=2 * 4 * vol.size, transcendentals=0),
    )(halo, vol, kbig, pair)


def backward_rows(pair_ref, *refs):
    groups = len(refs) - 4
    recv_refs = refs[:groups - 1]
    own_ref, k_ref, out_ref, resp_ref, up_ref = refs[groups - 1:]
    planes, rows_out, share, cols_out = pair_ref.shape
    rows = out_ref.shape[1]
    cols = out_ref.shape[3]
    total = own_ref[...]
    for recv_ref in recv_refs:
        total = total + recv_ref[0]
    resp_ref[...] = total.astype(resp_ref.dtype)
    tsel = spread_matrix(cols_out, cols, True)
    for q in range(groups):
        if q == 0:
            piece = pair_ref[...]
        else:
            piece = recv_refs[groups - q - 1][1:].astype(up_ref.dtype)
        flat = piece.reshape(planes * rows_out * share, cols_out)
        spread = jnp.dot(flat, tsel, preferred_element_type=jnp.float32)
        up_ref[:, :, q * share:(q + 1) * share, :] = spread.astype(up_ref.dtype).reshape(planes, rows_out, share, 3 * cols)
    for depth in range(2):
        sources = [(1, 0)] if depth == 0 else [(2, 0), (0, 1)]
        for row in range(rows):
            weights, values = [], []
            for depth_tap, plane in sources:
                for row_tap in range(3):
                    if (row + 1 - row_tap) % 2:
                        continue
                    i = (row + 1 - row_tap) // 2
                    if not 0 <= i < rows_out:
                        continue
                    for col_tap in range(3):
                        weights.append(k_ref[9 * depth_tap + 3 * row_tap + col_tap])
                        values.append(up_ref[plane, i, :, col_tap * cols:(col_tap + 1) * cols])
            lhs = jnp.concatenate(weights, axis=1)
            rhs = jnp.concatenate(values, axis=0)
            out_ref[depth, row] = jnp.dot(lhs, rhs, preferred_element_type=jnp.float32).astype(out_ref.dtype)


def backward_grad(pair, received, own, kernel):
    planes, rows_out, share, cols_out = pair.shape
    groups = len(received) + 1
    chans_out = share * groups
    taps, chans, _ = kernel.shape
    rows, cols = 2 * rows_out, 2 * cols_out
    flops = 2 * planes * rows_out * chans_out * cols_out * 3 * cols + 2 * 2 * rows * chans * 9 * chans_out * cols
    return pl.pallas_call(
        backward_rows,
        out_shape=[
            jax.ShapeDtypeStruct((2, rows, chans, cols), kernel.dtype),
            jax.ShapeDtypeStruct(own.shape, kernel.dtype),
        ],
        in_specs=[pl.BlockSpec(memory_space=pltpu.VMEM)] * (groups + 2),
        out_specs=[pl.BlockSpec(memory_space=pltpu.VMEM)] * 2,
        scratch_shapes=[pltpu.VMEM((planes, rows_out, chans_out, 3 * cols), kernel.dtype)],
        cost_estimate=pl.CostEstimate(flops=flops, bytes_accessed=2 * planes * rows_out * chans_out * cols_out + 2 * 2 * rows * chans * cols, transcendentals=0),
    )(pair, *received, own, kernel)


def chan_shift(block, shift):
    size = lax.axis_size("chan")
    return lax.ppermute(block, "chan", [(i, (i + shift) % size) for i in range(size)])


def per_device(volume, kernel, cotangent):
    count, planes_in, rows_in, chans_in, cols_in = volume.shape
    planes_out = planes_in // 2
    rows_out = rows_in // 2
    cols_out = cols_in // 2
    chans_out = kernel.shape[2]
    groups = lax.axis_size("chan")
    share = chans_out // groups
    me = lax.axis_index("chan")
    kernel = jnp.roll(kernel, -me * share, axis=2)
    below = from_behind(volume[:, -1:], "space", 1)
    pair = jnp.concatenate([cotangent, from_behind(cotangent, "space", -1)], axis=1)[0]
    own, *sent = forward_partial(below[0, 0], volume[0], kernel, pair, groups)
    received = [chan_shift(block, k) for k, block in enumerate(sent, start=1)]
    volume_grad, response = backward_grad(pair, received, own, kernel)
    response = response.reshape(count, planes_out, rows_out, share, cols_out)
    volume_grad = volume_grad.reshape(count, planes_in, rows_in, chans_in, cols_in)
    return (response, volume_grad)


def solution(mesh):
    placed = (
        P("dp", "space", None, "chan", None),
        P(None, "chan", None),
        P("dp", "space", None, "chan", None),
    )
    return jax.shard_map(
        per_device,
        mesh=mesh,
        in_specs=placed,
        out_specs=(P("dp", "space", None, "chan", None), P("dp", "space", None, "chan", None)),
        check_vma=False,
    )
```

```python
import jax
import jax.numpy as jnp
from jax import lax
from jax.sharding import PartitionSpec as P
from jax.experimental import pallas as pl
from jax.experimental.pallas import tpu as pltpu


def from_behind(block, axis, distance):
    devices = range(lax.axis_size(axis))
    route = [(i - distance, i) for i in devices if i - distance in devices]
    return lax.ppermute(block, axis, route)


def shift_front(values, axis):
    widths = [(0, 0)] * values.ndim
    widths[axis] = (1, 0)
    return jnp.pad(lax.slice_in_dim(values, 0, values.shape[axis] - 1, 1, axis), widths)


def shift_back(values, axis):
    widths = [(0, 0)] * values.ndim
    widths[axis] = (0, 1)
    return jnp.pad(lax.slice_in_dim(values, 1, values.shape[axis], 1, axis), widths)


def transposed_phases(source, taps):
    shift_row = shift_back(source, 2)
    shift_col = shift_back(source, 4)
    shift_both = shift_back(shift_row, 4)
    sources = {(0, 0): source, (1, 0): shift_row, (0, 1): shift_col, (1, 1): shift_both}
    phases = {}
    for row_tap in range(3):
        for col_tap in range(3):
            picked = sources[int(row_tap == 0), int(col_tap == 0)]
            term = jnp.einsum(
                "bdhew,ce->bdhcw",
                picked,
                taps[row_tap, col_tap],
                preferred_element_type=jnp.float32,
            )
            place = (0 if row_tap == 1 else 1, 0 if col_tap == 1 else 1)
            phases[place] = term if place not in phases else phases[place] + term
    upper = jnp.stack([phases[0, 0], phases[0, 1]], axis=4)
    lower = jnp.stack([phases[1, 0], phases[1, 1]], axis=4)
    return jnp.stack([upper, lower], axis=3)


def spread_matrix(rows, cols, transposed):
    blocks = []
    for tap in range(3):
        narrow = lax.broadcasted_iota(jnp.int32, (rows, cols), 1 if not transposed else 0)
        wide = lax.broadcasted_iota(jnp.int32, (rows, cols), 0 if not transposed else 1)
        blocks.append(jnp.where(wide == 2 * narrow + tap - 1, 1.0, 0.0).astype(jnp.bfloat16))
    return jnp.concatenate(blocks, axis=1)


def forward_rows(halo_ref, vol_ref, kbig_ref, *refs):
    out_refs, picked_ref = refs[:-1], refs[-1]
    planes, rows, chans, cols = vol_ref.shape
    rows_out, share, cols_out = out_refs[0].shape
    sel = spread_matrix(cols, cols_out, False)
    for plane in range(planes + 1):
        source = halo_ref[...] if plane == 0 else vol_ref[plane - 1]
        flat = source.reshape(rows * chans, cols)
        chosen = jnp.dot(flat, sel, preferred_element_type=jnp.float32)
        picked_ref[plane] = chosen.astype(picked_ref.dtype).reshape(rows, chans, 3 * cols_out)
    kbig = kbig_ref[...]
    zero = jnp.zeros((chans, cols_out), picked_ref.dtype)
    for i in range(rows_out):
        pieces = []
        for depth_tap in range(3):
            for row_tap in range(3):
                row = 2 * i + row_tap - 1
                for col_tap in range(3):
                    if row < 0:
                        pieces.append(zero)
                    else:
                        pieces.append(picked_ref[depth_tap, row, :, col_tap * cols_out:(col_tap + 1) * cols_out])
        stacked = jnp.concatenate(pieces, axis=0)
        result = jnp.dot(kbig, stacked, preferred_element_type=jnp.float32)
        for k, out_ref in enumerate(out_refs):
            out_ref[i] = result[k * share:(k + 1) * share]


def forward_partial(halo, vol, kernel, groups):
    planes, rows, chans, cols = vol.shape
    taps, _, chans_out = kernel.shape
    rows_out, cols_out = rows // 2, cols // 2
    share = chans_out // groups
    kbig = jnp.transpose(kernel, (2, 0, 1)).reshape(chans_out, taps * chans)
    flops = 2 * (planes + 1) * rows * chans * cols * 3 * cols_out + 2 * rows_out * chans_out * taps * chans * cols_out
    return pl.pallas_call(
        forward_rows,
        out_shape=[jax.ShapeDtypeStruct((rows_out, share, cols_out), jnp.float32)] * groups,
        in_specs=[pl.BlockSpec(memory_space=pltpu.VMEM)] * 3,
        out_specs=[pl.BlockSpec(memory_space=pltpu.VMEM)] * groups,
        scratch_shapes=[pltpu.VMEM((planes + 1, rows, chans, 3 * cols_out), vol.dtype)],
        cost_estimate=pl.CostEstimate(flops=flops, bytes_accessed=2 * 4 * vol.size, transcendentals=0),
    )(halo, vol, kbig)


def backward_rows(*refs):
    groups = len(refs) - 4
    cot_refs, next_ref, k_ref, out_ref, up_ref = refs[:groups], refs[groups], refs[groups + 1], refs[groups + 2], refs[groups + 3]
    rows_out, share, cols_out = cot_refs[0].shape
    chans_out = next_ref.shape[1]
    rows = out_ref.shape[1]
    cols = out_ref.shape[3]
    tsel = spread_matrix(cols_out, cols, True)
    for k, cot_ref in enumerate(cot_refs):
        flat = cot_ref[...].reshape(rows_out * share, cols_out)
        spread = jnp.dot(flat, tsel, preferred_element_type=jnp.float32)
        up_ref[0, :, k * share:(k + 1) * share, :] = spread.astype(up_ref.dtype).reshape(rows_out, share, 3 * cols)
    flat = next_ref[...].reshape(rows_out * chans_out, cols_out)
    spread = jnp.dot(flat, tsel, preferred_element_type=jnp.float32)
    up_ref[1] = spread.astype(up_ref.dtype).reshape(rows_out, chans_out, 3 * cols)
    for depth in range(2):
        sources = [(1, 0)] if depth == 0 else [(2, 0), (0, 1)]
        for row in range(rows):
            weights, values = [], []
            for depth_tap, plane in sources:
                for row_tap in range(3):
                    if (row + 1 - row_tap) % 2:
                        continue
                    i = (row + 1 - row_tap) // 2
                    if not 0 <= i < rows_out:
                        continue
                    for col_tap in range(3):
                        weights.append(k_ref[9 * depth_tap + 3 * row_tap + col_tap])
                        values.append(up_ref[plane, i, :, col_tap * cols:(col_tap + 1) * cols])
            lhs = jnp.concatenate(weights, axis=1)
            rhs = jnp.concatenate(values, axis=0)
            out_ref[depth, row] = jnp.dot(lhs, rhs, preferred_element_type=jnp.float32).astype(out_ref.dtype)


def backward_grad(pieces, following, kernel):
    planes = 2
    rows_out, share, cols_out = pieces[0].shape
    chans_out = share * len(pieces)
    taps, chans, _ = kernel.shape
    rows, cols = 2 * rows_out, 2 * cols_out
    flops = 2 * planes * rows_out * chans_out * cols_out * 3 * cols + 2 * 2 * rows * chans * 9 * chans_out * cols
    return pl.pallas_call(
        backward_rows,
        out_shape=jax.ShapeDtypeStruct((2, rows, chans, cols), kernel.dtype),
        in_specs=[pl.BlockSpec(memory_space=pltpu.VMEM)] * (len(pieces) + 2),
        out_specs=pl.BlockSpec(memory_space=pltpu.VMEM),
        scratch_shapes=[pltpu.VMEM((planes, rows_out, chans_out, 3 * cols), kernel.dtype)],
        cost_estimate=pl.CostEstimate(flops=flops, bytes_accessed=2 * planes * rows_out * chans_out * cols_out + 2 * 2 * rows * chans * cols, transcendentals=0),
    )(*pieces, following, kernel)


def chan_shift(block, shift):
    size = lax.axis_size("chan")
    return lax.ppermute(block, "chan", [(i, (i + shift) % size) for i in range(size)])


def per_device(volume, kernel, cotangent):
    count, planes_in, rows_in, chans_in, cols_in = volume.shape
    planes_out = planes_in // 2
    rows_out = rows_in // 2
    cols_out = cols_in // 2
    chans_out = kernel.shape[2]
    groups = lax.axis_size("chan")
    share = chans_out // groups
    me = lax.axis_index("chan")
    kernel = jnp.roll(kernel, -me * share, axis=2)
    own = cotangent[0, 0]
    pieces = [own] + [chan_shift(own, -k) for k in range(1, groups)]
    below = from_behind(volume[:, -1:], "space", 1)
    pieces, below = lax.optimization_barrier((pieces, below))
    chunks = forward_partial(below[0, 0], volume[0], kernel, groups)
    total = chunks[0]
    for k in range(1, groups):
        total = total + chan_shift(chunks[k], k)
    response = total.astype(jnp.bfloat16).reshape(count, planes_out, rows_out, share, cols_out)
    following = from_behind(jnp.concatenate(pieces, axis=1), "space", -1)
    volume_grad = backward_grad(pieces, following, kernel).reshape(count, planes_in, rows_in, chans_in, cols_in)
    return (response, volume_grad)


def solution(mesh):
    placed = (
        P("dp", "space", None, "chan", None),
        P(None, "chan", None),
        P("dp", "space", None, "chan", None),
    )
    return jax.shard_map(
        per_device,
        mesh=mesh,
        in_specs=placed,
        out_specs=(P("dp", "space", None, "chan", None), P("dp", "space", None, "chan", None)),
        check_vma=False,
    )
```

```python
import jax
import jax.numpy as jnp
from jax import lax
from jax.sharding import PartitionSpec as P
from jax.experimental import pallas as pl
from jax.experimental.pallas import tpu as pltpu


def from_behind(block, axis, distance):
    devices = range(lax.axis_size(axis))
    route = [(i - distance, i) for i in devices if i - distance in devices]
    return lax.ppermute(block, axis, route)


def shift_front(values, axis):
    widths = [(0, 0)] * values.ndim
    widths[axis] = (1, 0)
    return jnp.pad(lax.slice_in_dim(values, 0, values.shape[axis] - 1, 1, axis), widths)


def shift_back(values, axis):
    widths = [(0, 0)] * values.ndim
    widths[axis] = (0, 1)
    return jnp.pad(lax.slice_in_dim(values, 1, values.shape[axis], 1, axis), widths)


def transposed_phases(source, taps):
    shift_row = shift_back(source, 2)
    shift_col = shift_back(source, 4)
    shift_both = shift_back(shift_row, 4)
    sources = {(0, 0): source, (1, 0): shift_row, (0, 1): shift_col, (1, 1): shift_both}
    phases = {}
    for row_tap in range(3):
        for col_tap in range(3):
            picked = sources[int(row_tap == 0), int(col_tap == 0)]
            term = jnp.einsum(
                "bdhew,ce->bdhcw",
                picked,
                taps[row_tap, col_tap],
                preferred_element_type=jnp.float32,
            )
            place = (0 if row_tap == 1 else 1, 0 if col_tap == 1 else 1)
            phases[place] = term if place not in phases else phases[place] + term
    upper = jnp.stack([phases[0, 0], phases[0, 1]], axis=4)
    lower = jnp.stack([phases[1, 0], phases[1, 1]], axis=4)
    return jnp.stack([upper, lower], axis=3)


def spread_matrix(rows, cols, transposed):
    blocks = []
    for tap in range(3):
        narrow = lax.broadcasted_iota(jnp.int32, (rows, cols), 1 if not transposed else 0)
        wide = lax.broadcasted_iota(jnp.int32, (rows, cols), 0 if not transposed else 1)
        blocks.append(jnp.where(wide == 2 * narrow + tap - 1, 1.0, 0.0).astype(jnp.bfloat16))
    return jnp.concatenate(blocks, axis=1)


def forward_rows(halo_ref, vol_ref, kbig_ref, *refs):
    out_refs, picked_ref = refs[:-1], refs[-1]
    planes, rows, chans, cols = vol_ref.shape
    rows_out, share, cols_out = out_refs[0].shape
    sel = spread_matrix(cols, cols_out, False)
    for plane in range(planes + 1):
        source = halo_ref[...] if plane == 0 else vol_ref[plane - 1]
        flat = source.reshape(rows * chans, cols)
        chosen = jnp.dot(flat, sel, preferred_element_type=jnp.float32)
        picked_ref[plane] = chosen.astype(picked_ref.dtype).reshape(rows, chans, 3 * cols_out)
    kbig = kbig_ref[...]
    zero = jnp.zeros((chans, cols_out), picked_ref.dtype)
    for i in range(rows_out):
        pieces = []
        for depth_tap in range(3):
            for row_tap in range(3):
                row = 2 * i + row_tap - 1
                for col_tap in range(3):
                    if row < 0:
                        pieces.append(zero)
                    else:
                        pieces.append(picked_ref[depth_tap, row, :, col_tap * cols_out:(col_tap + 1) * cols_out])
        stacked = jnp.concatenate(pieces, axis=0)
        result = jnp.dot(kbig, stacked, preferred_element_type=jnp.float32)
        for k, out_ref in enumerate(out_refs):
            out_ref[i] = result[k * share:(k + 1) * share]


def forward_partial(halo, vol, kernel, groups):
    planes, rows, chans, cols = vol.shape
    taps, _, chans_out = kernel.shape
    rows_out, cols_out = rows // 2, cols // 2
    share = chans_out // groups
    kbig = jnp.transpose(kernel, (2, 0, 1)).reshape(chans_out, taps * chans)
    flops = 2 * (planes + 1) * rows * chans * cols * 3 * cols_out + 2 * rows_out * chans_out * taps * chans * cols_out
    return pl.pallas_call(
        forward_rows,
        out_shape=[jax.ShapeDtypeStruct((rows_out, share, cols_out), jnp.float32)] * groups,
        in_specs=[pl.BlockSpec(memory_space=pltpu.VMEM)] * 3,
        out_specs=[pl.BlockSpec(memory_space=pltpu.VMEM)] * groups,
        scratch_shapes=[pltpu.VMEM((planes + 1, rows, chans, 3 * cols_out), vol.dtype)],
        cost_estimate=pl.CostEstimate(flops=flops, bytes_accessed=2 * 4 * vol.size, transcendentals=0),
    )(halo, vol, kbig)


def backward_rows(*refs):
    count = len(refs) - 3
    cot_refs, k_ref, out_ref, up_ref = refs[:count], refs[count], refs[count + 1], refs[count + 2]
    planes = 2
    groups = count // planes
    rows_out, share, cols_out = cot_refs[0].shape
    rows = out_ref.shape[1]
    cols = out_ref.shape[3]
    tsel = spread_matrix(cols_out, cols, True)
    for n, cot_ref in enumerate(cot_refs):
        plane, k = divmod(n, groups)
        flat = cot_ref[...].reshape(rows_out * share, cols_out)
        spread = jnp.dot(flat, tsel, preferred_element_type=jnp.float32)
        up_ref[plane, :, k * share:(k + 1) * share, :] = spread.astype(up_ref.dtype).reshape(rows_out, share, 3 * cols)
    for depth in range(2):
        sources = [(1, 0)] if depth == 0 else [(2, 0), (0, 1)]
        for row in range(rows):
            weights, values = [], []
            for depth_tap, plane in sources:
                for row_tap in range(3):
                    if (row + 1 - row_tap) % 2:
                        continue
                    i = (row + 1 - row_tap) // 2
                    if not 0 <= i < rows_out:
                        continue
                    for col_tap in range(3):
                        weights.append(k_ref[9 * depth_tap + 3 * row_tap + col_tap])
                        values.append(up_ref[plane, i, :, col_tap * cols:(col_tap + 1) * cols])
            lhs = jnp.concatenate(weights, axis=1)
            rhs = jnp.concatenate(values, axis=0)
            out_ref[depth, row] = jnp.dot(lhs, rhs, preferred_element_type=jnp.float32).astype(out_ref.dtype)


def backward_grad(pieces, kernel):
    planes = 2
    rows_out, share, cols_out = pieces[0].shape
    chans_out = share * len(pieces) // planes
    taps, chans, _ = kernel.shape
    rows, cols = 2 * rows_out, 2 * cols_out
    flops = 2 * planes * rows_out * chans_out * cols_out * 3 * cols + 2 * 2 * rows * chans * 9 * chans_out * cols
    return pl.pallas_call(
        backward_rows,
        out_shape=jax.ShapeDtypeStruct((2, rows, chans, cols), kernel.dtype),
        in_specs=[pl.BlockSpec(memory_space=pltpu.VMEM)] * (len(pieces) + 1),
        out_specs=pl.BlockSpec(memory_space=pltpu.VMEM),
        scratch_shapes=[pltpu.VMEM((planes, rows_out, chans_out, 3 * cols), kernel.dtype)],
        cost_estimate=pl.CostEstimate(flops=flops, bytes_accessed=2 * planes * rows_out * chans_out * cols_out + 2 * 2 * rows * chans * cols, transcendentals=0),
    )(*pieces, kernel)


def chan_shift(block, shift):
    size = lax.axis_size("chan")
    return lax.ppermute(block, "chan", [(i, (i + shift) % size) for i in range(size)])


def per_device(volume, kernel, cotangent):
    count, planes_in, rows_in, chans_in, cols_in = volume.shape
    planes_out = planes_in // 2
    rows_out = rows_in // 2
    cols_out = cols_in // 2
    chans_out = kernel.shape[2]
    groups = lax.axis_size("chan")
    share = chans_out // groups
    me = lax.axis_index("chan")
    kernel = jnp.roll(kernel, -me * share, axis=2)
    own = cotangent[0, 0]
    own_pieces = [own] + [chan_shift(own, -k) for k in range(1, groups)]
    following = from_behind(cotangent, "space", -1)[0, 0]
    below = from_behind(volume[:, -1:], "space", 1)
    own_pieces, below = lax.optimization_barrier((own_pieces, below))
    chunks = forward_partial(below[0, 0], volume[0], kernel, groups)
    chunks, following = lax.optimization_barrier((chunks, following))
    total = chunks[0]
    for k in range(1, groups):
        total = total + chan_shift(chunks[k], k)
    response = total.astype(jnp.bfloat16).reshape(count, planes_out, rows_out, share, cols_out)
    pieces = own_pieces + [following] + [chan_shift(following, -k) for k in range(1, groups)]
    volume_grad = backward_grad(pieces, kernel).reshape(count, planes_in, rows_in, chans_in, cols_in)
    return (response, volume_grad)


def solution(mesh):
    placed = (
        P("dp", "space", None, "chan", None),
        P(None, "chan", None),
        P("dp", "space", None, "chan", None),
    )
    return jax.shard_map(
        per_device,
        mesh=mesh,
        in_specs=placed,
        out_specs=(P("dp", "space", None, "chan", None), P("dp", "space", None, "chan", None)),
        check_vma=False,
    )
```

```python
import jax
import jax.numpy as jnp
from jax import lax
from jax.sharding import PartitionSpec as P
from jax.experimental import pallas as pl
from jax.experimental.pallas import tpu as pltpu


def from_behind(block, axis, distance):
    devices = range(lax.axis_size(axis))
    route = [(i - distance, i) for i in devices if i - distance in devices]
    return lax.ppermute(block, axis, route)


def shift_front(values, axis):
    widths = [(0, 0)] * values.ndim
    widths[axis] = (1, 0)
    return jnp.pad(lax.slice_in_dim(values, 0, values.shape[axis] - 1, 1, axis), widths)


def shift_back(values, axis):
    widths = [(0, 0)] * values.ndim
    widths[axis] = (0, 1)
    return jnp.pad(lax.slice_in_dim(values, 1, values.shape[axis], 1, axis), widths)


def transposed_phases(source, taps):
    shift_row = shift_back(source, 2)
    shift_col = shift_back(source, 4)
    shift_both = shift_back(shift_row, 4)
    sources = {(0, 0): source, (1, 0): shift_row, (0, 1): shift_col, (1, 1): shift_both}
    phases = {}
    for row_tap in range(3):
        for col_tap in range(3):
            picked = sources[int(row_tap == 0), int(col_tap == 0)]
            term = jnp.einsum(
                "bdhew,ce->bdhcw",
                picked,
                taps[row_tap, col_tap],
                preferred_element_type=jnp.float32,
            )
            place = (0 if row_tap == 1 else 1, 0 if col_tap == 1 else 1)
            phases[place] = term if place not in phases else phases[place] + term
    upper = jnp.stack([phases[0, 0], phases[0, 1]], axis=4)
    lower = jnp.stack([phases[1, 0], phases[1, 1]], axis=4)
    return jnp.stack([upper, lower], axis=3)


def spread_matrix(rows, cols, transposed):
    blocks = []
    for tap in range(3):
        narrow = lax.broadcasted_iota(jnp.int32, (rows, cols), 1 if not transposed else 0)
        wide = lax.broadcasted_iota(jnp.int32, (rows, cols), 0 if not transposed else 1)
        blocks.append(jnp.where(wide == 2 * narrow + tap - 1, 1.0, 0.0).astype(jnp.bfloat16))
    return jnp.concatenate(blocks, axis=1)


def forward_taps(source_refs, kbig_ref, acc_ref, out_refs, picked_ref, first_tap):
    planes = len(source_refs)
    rows, chans, cols = source_refs[0].shape
    rows_out, cols_out = rows // 2, cols // 2
    share = out_refs[0].shape[1]
    sel = spread_matrix(cols, cols_out, False)
    for plane, source_ref in enumerate(source_refs):
        flat = source_ref[...].reshape(rows * chans, cols)
        chosen = jnp.dot(flat, sel, preferred_element_type=jnp.float32)
        picked_ref[plane] = chosen.astype(picked_ref.dtype).reshape(rows, chans, 3 * cols_out)
    kpart = kbig_ref[:, first_tap * 9 * chans:(first_tap + planes) * 9 * chans]
    zero = jnp.zeros((chans, cols_out), picked_ref.dtype)
    for i in range(rows_out):
        pieces = []
        for plane in range(planes):
            for row_tap in range(3):
                row = 2 * i + row_tap - 1
                for col_tap in range(3):
                    if row < 0:
                        pieces.append(zero)
                    else:
                        pieces.append(picked_ref[plane, row, :, col_tap * cols_out:(col_tap + 1) * cols_out])
        stacked = jnp.concatenate(pieces, axis=0)
        result = jnp.dot(kpart, stacked, preferred_element_type=jnp.float32)
        if acc_ref is not None:
            result = acc_ref[i] + result
        if len(out_refs) == 1 and share == result.shape[0]:
            out_refs[0][i] = result
        else:
            for k, out_ref in enumerate(out_refs):
                out_ref[i] = result[k * share:(k + 1) * share]


def forward_local_rows(vol_ref, kbig_ref, acc_ref, picked_ref):
    forward_taps([vol_ref.at[0], vol_ref.at[1]], kbig_ref, None, [acc_ref], picked_ref, 1)


def forward_halo_rows(halo_ref, acc_ref, kbig_ref, *refs):
    out_refs, picked_ref = refs[:-1], refs[-1]
    forward_taps([halo_ref], kbig_ref, acc_ref, list(out_refs), picked_ref, 0)


def forward_partial(halo, vol, kernel, groups):
    planes, rows, chans, cols = vol.shape
    taps, _, chans_out = kernel.shape
    rows_out, cols_out = rows // 2, cols // 2
    share = chans_out // groups
    kbig = jnp.transpose(kernel, (2, 0, 1)).reshape(chans_out, taps * chans)
    vmem = pl.BlockSpec(memory_space=pltpu.VMEM)
    per_plane = 2 * rows * chans * cols * 3 * cols_out + 2 * rows_out * chans_out * 9 * chans * cols_out
    acc = pl.pallas_call(
        forward_local_rows,
        out_shape=jax.ShapeDtypeStruct((rows_out, chans_out, cols_out), jnp.float32),
        in_specs=[vmem] * 2,
        out_specs=vmem,
        scratch_shapes=[pltpu.VMEM((planes, rows, chans, 3 * cols_out), vol.dtype)],
        cost_estimate=pl.CostEstimate(flops=planes * per_plane, bytes_accessed=2 * vol.size + 4 * rows_out * chans_out * cols_out, transcendentals=0),
    )(vol, kbig)
    return pl.pallas_call(
        forward_halo_rows,
        out_shape=[jax.ShapeDtypeStruct((rows_out, share, cols_out), jnp.float32)] * groups,
        in_specs=[vmem] * 3,
        out_specs=[vmem] * groups,
        scratch_shapes=[pltpu.VMEM((1, rows, chans, 3 * cols_out), vol.dtype)],
        cost_estimate=pl.CostEstimate(flops=per_plane, bytes_accessed=2 * halo.size + 8 * rows_out * chans_out * cols_out, transcendentals=0),
    )(halo, acc, kbig)


def backward_rows(*refs):
    groups = (len(refs) - 3)
    cot_refs, k_ref, out_ref, up_ref = refs[:groups], refs[groups], refs[groups + 1], refs[groups + 2]
    planes, rows_out, share, cols_out = cot_refs[0].shape
    rows = out_ref.shape[1]
    cols = out_ref.shape[3]
    tsel = spread_matrix(cols_out, cols, True)
    for k, cot_ref in enumerate(cot_refs):
        flat = cot_ref[...].reshape(planes * rows_out * share, cols_out)
        spread = jnp.dot(flat, tsel, preferred_element_type=jnp.float32)
        up_ref[:, :, k * share:(k + 1) * share, :] = spread.astype(up_ref.dtype).reshape(planes, rows_out, share, 3 * cols)
    for depth in range(2):
        sources = [(1, 0)] if depth == 0 else [(2, 0), (0, 1)]
        for row in range(rows):
            weights, values = [], []
            for depth_tap, plane in sources:
                for row_tap in range(3):
                    if (row + 1 - row_tap) % 2:
                        continue
                    i = (row + 1 - row_tap) // 2
                    if not 0 <= i < rows_out:
                        continue
                    for col_tap in range(3):
                        weights.append(k_ref[9 * depth_tap + 3 * row_tap + col_tap])
                        values.append(up_ref[plane, i, :, col_tap * cols:(col_tap + 1) * cols])
            lhs = jnp.concatenate(weights, axis=1)
            rhs = jnp.concatenate(values, axis=0)
            out_ref[depth, row] = jnp.dot(lhs, rhs, preferred_element_type=jnp.float32).astype(out_ref.dtype)


def backward_grad(pieces, kernel):
    planes, rows_out, share, cols_out = pieces[0].shape
    chans_out = share * len(pieces)
    taps, chans, _ = kernel.shape
    rows, cols = 2 * rows_out, 2 * cols_out
    flops = 2 * planes * rows_out * chans_out * cols_out * 3 * cols + 2 * 2 * rows * chans * 9 * chans_out * cols
    return pl.pallas_call(
        backward_rows,
        out_shape=jax.ShapeDtypeStruct((2, rows, chans, cols), kernel.dtype),
        in_specs=[pl.BlockSpec(memory_space=pltpu.VMEM)] * (len(pieces) + 1),
        out_specs=pl.BlockSpec(memory_space=pltpu.VMEM),
        scratch_shapes=[pltpu.VMEM((planes, rows_out, chans_out, 3 * cols), kernel.dtype)],
        cost_estimate=pl.CostEstimate(flops=flops, bytes_accessed=2 * planes * rows_out * chans_out * cols_out + 2 * 2 * rows * chans * cols, transcendentals=0),
    )(*pieces, kernel)


def chan_shift(block, shift):
    size = lax.axis_size("chan")
    return lax.ppermute(block, "chan", [(i, (i + shift) % size) for i in range(size)])


def per_device(volume, kernel, cotangent):
    count, planes_in, rows_in, chans_in, cols_in = volume.shape
    planes_out = planes_in // 2
    rows_out = rows_in // 2
    cols_out = cols_in // 2
    chans_out = kernel.shape[2]
    groups = lax.axis_size("chan")
    share = chans_out // groups
    me = lax.axis_index("chan")
    kernel = jnp.roll(kernel, -me * share, axis=2)
    below = from_behind(volume[:, -1:], "space", 1)
    chunks = forward_partial(below[0, 0], volume[0], kernel, groups)
    pair = jnp.concatenate([cotangent, from_behind(cotangent, "space", -1)], axis=1)
    chunks, pair = lax.optimization_barrier((chunks, pair))
    total = chunks[0]
    for k in range(1, groups):
        total = total + chan_shift(chunks[k], k)
    response = total.astype(jnp.bfloat16).reshape(count, planes_out, rows_out, share, cols_out)
    pieces = [pair[0]] + [chan_shift(pair[0], -k) for k in range(1, groups)]
    volume_grad = backward_grad(pieces, kernel).reshape(count, planes_in, rows_in, chans_in, cols_in)
    return (response, volume_grad)


def solution(mesh):
    placed = (
        P("dp", "space", None, "chan", None),
        P(None, "chan", None),
        P("dp", "space", None, "chan", None),
    )
    return jax.shard_map(
        per_device,
        mesh=mesh,
        in_specs=placed,
        out_specs=(P("dp", "space", None, "chan", None), P("dp", "space", None, "chan", None)),
        check_vma=False,
    )
```

```python
import jax
import jax.numpy as jnp
from jax import lax
from jax.sharding import PartitionSpec as P
from jax.experimental import pallas as pl
from jax.experimental.pallas import tpu as pltpu


def from_behind(block, axis, distance):
    devices = range(lax.axis_size(axis))
    route = [(i - distance, i) for i in devices if i - distance in devices]
    return lax.ppermute(block, axis, route)


def shift_front(values, axis):
    widths = [(0, 0)] * values.ndim
    widths[axis] = (1, 0)
    return jnp.pad(lax.slice_in_dim(values, 0, values.shape[axis] - 1, 1, axis), widths)


def shift_back(values, axis):
    widths = [(0, 0)] * values.ndim
    widths[axis] = (0, 1)
    return jnp.pad(lax.slice_in_dim(values, 1, values.shape[axis], 1, axis), widths)


def transposed_phases(source, taps):
    shift_row = shift_back(source, 2)
    shift_col = shift_back(source, 4)
    shift_both = shift_back(shift_row, 4)
    sources = {(0, 0): source, (1, 0): shift_row, (0, 1): shift_col, (1, 1): shift_both}
    phases = {}
    for row_tap in range(3):
        for col_tap in range(3):
            picked = sources[int(row_tap == 0), int(col_tap == 0)]
            term = jnp.einsum(
                "bdhew,ce->bdhcw",
                picked,
                taps[row_tap, col_tap],
                preferred_element_type=jnp.float32,
            )
            place = (0 if row_tap == 1 else 1, 0 if col_tap == 1 else 1)
            phases[place] = term if place not in phases else phases[place] + term
    upper = jnp.stack([phases[0, 0], phases[0, 1]], axis=4)
    lower = jnp.stack([phases[1, 0], phases[1, 1]], axis=4)
    return jnp.stack([upper, lower], axis=3)


def spread_matrix(rows, cols, transposed):
    blocks = []
    for tap in range(3):
        narrow = lax.broadcasted_iota(jnp.int32, (rows, cols), 1 if not transposed else 0)
        wide = lax.broadcasted_iota(jnp.int32, (rows, cols), 0 if not transposed else 1)
        blocks.append(jnp.where(wide == 2 * narrow + tap - 1, 1.0, 0.0).astype(jnp.bfloat16))
    return jnp.concatenate(blocks, axis=1)


def forward_taps(source_refs, kbig_ref, acc_ref, out_refs, picked_ref, first_tap):
    planes = len(source_refs)
    rows, chans, cols = source_refs[0].shape
    rows_out, cols_out = rows // 2, cols // 2
    share = out_refs[0].shape[1]
    sel = spread_matrix(cols, cols_out, False)
    for plane, source_ref in enumerate(source_refs):
        flat = source_ref[...].reshape(rows * chans, cols)
        chosen = jnp.dot(flat, sel, preferred_element_type=jnp.float32)
        picked_ref[plane] = chosen.astype(picked_ref.dtype).reshape(rows, chans, 3 * cols_out)
    kpart = kbig_ref[:, first_tap * 9 * chans:(first_tap + planes) * 9 * chans]
    zero = jnp.zeros((chans, cols_out), picked_ref.dtype)
    for i in range(rows_out):
        pieces = []
        for plane in range(planes):
            for row_tap in range(3):
                row = 2 * i + row_tap - 1
                for col_tap in range(3):
                    if row < 0:
                        pieces.append(zero)
                    else:
                        pieces.append(picked_ref[plane, row, :, col_tap * cols_out:(col_tap + 1) * cols_out])
        stacked = jnp.concatenate(pieces, axis=0)
        result = jnp.dot(kpart, stacked, preferred_element_type=jnp.float32)
        if acc_ref is not None:
            result = acc_ref[i] + result
        if len(out_refs) == 1 and share == result.shape[0]:
            out_refs[0][i] = result
        else:
            out_refs[0][i] = result[:share]
            out_refs[1][i] = result[2 * share:3 * share]
            out_refs[2][0, i] = result[share:2 * share]
            out_refs[2][1, i] = result[3 * share:]


def forward_local_rows(vol_ref, kbig_ref, acc_ref, picked_ref):
    forward_taps([vol_ref.at[0], vol_ref.at[1]], kbig_ref, None, [acc_ref], picked_ref, 1)


def forward_halo_rows(halo_ref, acc_ref, kbig_ref, *refs):
    out_refs, picked_ref = refs[:-1], refs[-1]
    forward_taps([halo_ref], kbig_ref, acc_ref, list(out_refs), picked_ref, 0)


def forward_partial(halo, vol, kernel, groups):
    planes, rows, chans, cols = vol.shape
    taps, _, chans_out = kernel.shape
    rows_out, cols_out = rows // 2, cols // 2
    share = chans_out // groups
    kbig = jnp.transpose(kernel, (2, 0, 1)).reshape(chans_out, taps * chans)
    vmem = pl.BlockSpec(memory_space=pltpu.VMEM)
    per_plane = 2 * rows * chans * cols * 3 * cols_out + 2 * rows_out * chans_out * 9 * chans * cols_out
    acc = pl.pallas_call(
        forward_local_rows,
        out_shape=jax.ShapeDtypeStruct((rows_out, chans_out, cols_out), jnp.float32),
        in_specs=[vmem] * 2,
        out_specs=vmem,
        scratch_shapes=[pltpu.VMEM((planes, rows, chans, 3 * cols_out), vol.dtype)],
        cost_estimate=pl.CostEstimate(flops=planes * per_plane, bytes_accessed=2 * vol.size + 4 * rows_out * chans_out * cols_out, transcendentals=0),
    )(vol, kbig)
    block = jax.ShapeDtypeStruct((rows_out, share, cols_out), jnp.float32)
    return pl.pallas_call(
        forward_halo_rows,
        out_shape=[block, block, jax.ShapeDtypeStruct((2, rows_out, share, cols_out), jnp.float32)],
        in_specs=[vmem] * 3,
        out_specs=[vmem] * 3,
        scratch_shapes=[pltpu.VMEM((1, rows, chans, 3 * cols_out), vol.dtype)],
        cost_estimate=pl.CostEstimate(flops=per_plane, bytes_accessed=2 * halo.size + 8 * rows_out * chans_out * cols_out, transcendentals=0),
    )(halo, acc, kbig)


def backward_rows(*refs):
    groups = (len(refs) - 3)
    cot_refs, k_ref, out_ref, up_ref = refs[:groups], refs[groups], refs[groups + 1], refs[groups + 2]
    planes, rows_out, share, cols_out = cot_refs[0].shape
    rows = out_ref.shape[1]
    cols = out_ref.shape[3]
    tsel = spread_matrix(cols_out, cols, True)
    for k, cot_ref in enumerate(cot_refs):
        flat = cot_ref[...].reshape(planes * rows_out * share, cols_out)
        spread = jnp.dot(flat, tsel, preferred_element_type=jnp.float32)
        up_ref[:, :, k * share:(k + 1) * share, :] = spread.astype(up_ref.dtype).reshape(planes, rows_out, share, 3 * cols)
    for depth in range(2):
        sources = [(1, 0)] if depth == 0 else [(2, 0), (0, 1)]
        for row in range(rows):
            weights, values = [], []
            for depth_tap, plane in sources:
                for row_tap in range(3):
                    if (row + 1 - row_tap) % 2:
                        continue
                    i = (row + 1 - row_tap) // 2
                    if not 0 <= i < rows_out:
                        continue
                    for col_tap in range(3):
                        weights.append(k_ref[9 * depth_tap + 3 * row_tap + col_tap])
                        values.append(up_ref[plane, i, :, col_tap * cols:(col_tap + 1) * cols])
            lhs = jnp.concatenate(weights, axis=1)
            rhs = jnp.concatenate(values, axis=0)
            out_ref[depth, row] = jnp.dot(lhs, rhs, preferred_element_type=jnp.float32).astype(out_ref.dtype)


def backward_grad(pieces, kernel):
    planes, rows_out, share, cols_out = pieces[0].shape
    chans_out = share * len(pieces)
    taps, chans, _ = kernel.shape
    rows, cols = 2 * rows_out, 2 * cols_out
    flops = 2 * planes * rows_out * chans_out * cols_out * 3 * cols + 2 * 2 * rows * chans * 9 * chans_out * cols
    return pl.pallas_call(
        backward_rows,
        out_shape=jax.ShapeDtypeStruct((2, rows, chans, cols), kernel.dtype),
        in_specs=[pl.BlockSpec(memory_space=pltpu.VMEM)] * (len(pieces) + 1),
        out_specs=pl.BlockSpec(memory_space=pltpu.VMEM),
        scratch_shapes=[pltpu.VMEM((planes, rows_out, chans_out, 3 * cols), kernel.dtype)],
        cost_estimate=pl.CostEstimate(flops=flops, bytes_accessed=2 * planes * rows_out * chans_out * cols_out + 2 * 2 * rows * chans * cols, transcendentals=0),
    )(*pieces, kernel)


def chan_swap(block, mask):
    size = lax.axis_size("chan")
    return lax.ppermute(block, "chan", [(i, i ^ mask) for i in range(size)])


def per_device(volume, kernel, cotangent):
    count, planes_in, rows_in, chans_in, cols_in = volume.shape
    planes_out = planes_in // 2
    rows_out = rows_in // 2
    cols_out = cols_in // 2
    chans_out = kernel.shape[2]
    groups = lax.axis_size("chan")
    share = chans_out // groups
    me = lax.axis_index("chan")
    kernel = jnp.concatenate(
        [lax.dynamic_slice_in_dim(kernel, (me ^ k) * share, share, axis=2) for k in range(groups)], axis=2
    )
    below = from_behind(volume[:, -1:], "space", 1)
    own_block, far_block, sent = forward_partial(below[0, 0], volume[0], kernel, groups)
    pair = jnp.concatenate([cotangent, from_behind(cotangent, "space", -1)], axis=1)[0]
    (own_block, far_block, sent), pair = lax.optimization_barrier(((own_block, far_block, sent), pair))
    near = chan_swap(sent, 1)
    across = chan_swap(pair, 2)
    far_sum = far_block + near[1]
    total = (own_block + near[0]) + chan_swap(far_sum, 2)
    response = total.astype(jnp.bfloat16).reshape(count, planes_out, rows_out, share, cols_out)
    other = chan_swap(jnp.stack([pair, across]), 1)
    pieces = [pair, other[0], across, other[1]]
    volume_grad = backward_grad(pieces, kernel).reshape(count, planes_in, rows_in, chans_in, cols_in)
    return (response, volume_grad)


def solution(mesh):
    placed = (
        P("dp", "space", None, "chan", None),
        P(None, "chan", None),
        P("dp", "space", None, "chan", None),
    )
    return jax.shard_map(
        per_device,
        mesh=mesh,
        in_specs=placed,
        out_specs=(P("dp", "space", None, "chan", None), P("dp", "space", None, "chan", None)),
        check_vma=False,
    )
```

```python
import jax
import jax.numpy as jnp
from jax import lax
from jax.sharding import PartitionSpec as P
from jax.experimental import pallas as pl
from jax.experimental.pallas import tpu as pltpu


def from_behind(block, axis, distance):
    devices = range(lax.axis_size(axis))
    route = [(i - distance, i) for i in devices if i - distance in devices]
    return lax.ppermute(block, axis, route)


def shift_front(values, axis):
    widths = [(0, 0)] * values.ndim
    widths[axis] = (1, 0)
    return jnp.pad(lax.slice_in_dim(values, 0, values.shape[axis] - 1, 1, axis), widths)


def shift_back(values, axis):
    widths = [(0, 0)] * values.ndim
    widths[axis] = (0, 1)
    return jnp.pad(lax.slice_in_dim(values, 1, values.shape[axis], 1, axis), widths)


def transposed_phases(source, taps):
    shift_row = shift_back(source, 2)
    shift_col = shift_back(source, 4)
    shift_both = shift_back(shift_row, 4)
    sources = {(0, 0): source, (1, 0): shift_row, (0, 1): shift_col, (1, 1): shift_both}
    phases = {}
    for row_tap in range(3):
        for col_tap in range(3):
            picked = sources[int(row_tap == 0), int(col_tap == 0)]
            term = jnp.einsum(
                "bdhew,ce->bdhcw",
                picked,
                taps[row_tap, col_tap],
                preferred_element_type=jnp.float32,
            )
            place = (0 if row_tap == 1 else 1, 0 if col_tap == 1 else 1)
            phases[place] = term if place not in phases else phases[place] + term
    upper = jnp.stack([phases[0, 0], phases[0, 1]], axis=4)
    lower = jnp.stack([phases[1, 0], phases[1, 1]], axis=4)
    return jnp.stack([upper, lower], axis=3)


def spread_matrix(rows, cols, transposed):
    blocks = []
    for tap in range(3):
        narrow = lax.broadcasted_iota(jnp.int32, (rows, cols), 1 if not transposed else 0)
        wide = lax.broadcasted_iota(jnp.int32, (rows, cols), 0 if not transposed else 1)
        blocks.append(jnp.where(wide == 2 * narrow + tap - 1, 1.0, 0.0).astype(jnp.bfloat16))
    return jnp.concatenate(blocks, axis=1)


def forward_taps(source_refs, kbig_ref, acc_ref, out_refs, picked_ref, first_tap):
    planes = len(source_refs)
    rows, chans, cols = source_refs[0].shape
    rows_out, cols_out = rows // 2, cols // 2
    share = out_refs[0].shape[1]
    sel = spread_matrix(cols, cols_out, False)
    for plane, source_ref in enumerate(source_refs):
        flat = source_ref[...].reshape(rows * chans, cols)
        chosen = jnp.dot(flat, sel, preferred_element_type=jnp.float32)
        picked_ref[plane] = chosen.astype(picked_ref.dtype).reshape(rows, chans, 3 * cols_out)
    kpart = kbig_ref[:, first_tap * 9 * chans:(first_tap + planes) * 9 * chans]
    zero = jnp.zeros((chans, cols_out), picked_ref.dtype)
    for i in range(rows_out):
        pieces = []
        for plane in range(planes):
            for row_tap in range(3):
                row = 2 * i + row_tap - 1
                for col_tap in range(3):
                    if row < 0:
                        pieces.append(zero)
                    else:
                        pieces.append(picked_ref[plane, row, :, col_tap * cols_out:(col_tap + 1) * cols_out])
        stacked = jnp.concatenate(pieces, axis=0)
        result = jnp.dot(kpart, stacked, preferred_element_type=jnp.float32)
        if acc_ref is not None:
            result = acc_ref[i] + result
        if len(out_refs) == 1 and share == result.shape[0]:
            out_refs[0][i] = result
        else:
            out_refs[0][i] = result[:share]
            out_refs[1][i] = result[2 * share:3 * share]
            out_refs[2][0, i] = result[share:2 * share]
            out_refs[2][1, i] = result[3 * share:]


def forward_local_rows(vol_ref, kbig_ref, acc_ref, picked_ref):
    forward_taps([vol_ref.at[0], vol_ref.at[1]], kbig_ref, None, [acc_ref], picked_ref, 1)


def forward_halo_rows(halo_ref, acc_ref, kbig_ref, *refs):
    out_refs, picked_ref = refs[:-1], refs[-1]
    forward_taps([halo_ref], kbig_ref, acc_ref, list(out_refs), picked_ref, 0)


def forward_partial(halo, vol, kernel, groups):
    planes, rows, chans, cols = vol.shape
    taps, _, chans_out = kernel.shape
    rows_out, cols_out = rows // 2, cols // 2
    share = chans_out // groups
    kbig = jnp.transpose(kernel, (2, 0, 1)).reshape(chans_out, taps * chans)
    vmem = pl.BlockSpec(memory_space=pltpu.VMEM)
    per_plane = 2 * rows * chans * cols * 3 * cols_out + 2 * rows_out * chans_out * 9 * chans * cols_out
    acc = pl.pallas_call(
        forward_local_rows,
        out_shape=jax.ShapeDtypeStruct((rows_out, chans_out, cols_out), jnp.float32),
        in_specs=[vmem] * 2,
        out_specs=vmem,
        scratch_shapes=[pltpu.VMEM((planes, rows, chans, 3 * cols_out), vol.dtype)],
        cost_estimate=pl.CostEstimate(flops=planes * per_plane, bytes_accessed=2 * vol.size + 4 * rows_out * chans_out * cols_out, transcendentals=0),
    )(vol, kbig)
    block = jax.ShapeDtypeStruct((rows_out, share, cols_out), jnp.float32)
    return pl.pallas_call(
        forward_halo_rows,
        out_shape=[block, block, jax.ShapeDtypeStruct((2, rows_out, share, cols_out), jnp.float32)],
        in_specs=[vmem] * 3,
        out_specs=[vmem] * 3,
        scratch_shapes=[pltpu.VMEM((1, rows, chans, 3 * cols_out), vol.dtype)],
        cost_estimate=pl.CostEstimate(flops=per_plane, bytes_accessed=2 * halo.size + 8 * rows_out * chans_out * cols_out, transcendentals=0),
    )(halo, acc, kbig)


def backward_rows(*refs):
    groups = (len(refs) - 3)
    cot_refs, k_ref, out_ref, up_ref = refs[:groups], refs[groups], refs[groups + 1], refs[groups + 2]
    planes, rows_out, share, cols_out = cot_refs[0].shape
    rows = out_ref.shape[1]
    cols = out_ref.shape[3]
    tsel = spread_matrix(cols_out, cols, True)
    for k, cot_ref in enumerate(cot_refs):
        flat = cot_ref[...].reshape(planes * rows_out * share, cols_out)
        spread = jnp.dot(flat, tsel, preferred_element_type=jnp.float32)
        up_ref[:, :, k * share:(k + 1) * share, :] = spread.astype(up_ref.dtype).reshape(planes, rows_out, share, 3 * cols)
    for depth in range(2):
        sources = [(1, 0)] if depth == 0 else [(2, 0), (0, 1)]
        for row in range(rows):
            weights, values = [], []
            for depth_tap, plane in sources:
                for row_tap in range(3):
                    if (row + 1 - row_tap) % 2:
                        continue
                    i = (row + 1 - row_tap) // 2
                    if not 0 <= i < rows_out:
                        continue
                    for col_tap in range(3):
                        weights.append(k_ref[9 * depth_tap + 3 * row_tap + col_tap])
                        values.append(up_ref[plane, i, :, col_tap * cols:(col_tap + 1) * cols])
            lhs = jnp.concatenate(weights, axis=1)
            rhs = jnp.concatenate(values, axis=0)
            out_ref[depth, row] = jnp.dot(lhs, rhs, preferred_element_type=jnp.float32).astype(out_ref.dtype)


def backward_grad(pieces, kernel):
    planes, rows_out, share, cols_out = pieces[0].shape
    chans_out = share * len(pieces)
    taps, chans, _ = kernel.shape
    rows, cols = 2 * rows_out, 2 * cols_out
    flops = 2 * planes * rows_out * chans_out * cols_out * 3 * cols + 2 * 2 * rows * chans * 9 * chans_out * cols
    return pl.pallas_call(
        backward_rows,
        out_shape=jax.ShapeDtypeStruct((2, rows, chans, cols), kernel.dtype),
        in_specs=[pl.BlockSpec(memory_space=pltpu.VMEM)] * (len(pieces) + 1),
        out_specs=pl.BlockSpec(memory_space=pltpu.VMEM),
        scratch_shapes=[pltpu.VMEM((planes, rows_out, chans_out, 3 * cols), kernel.dtype)],
        cost_estimate=pl.CostEstimate(flops=flops, bytes_accessed=2 * planes * rows_out * chans_out * cols_out + 2 * 2 * rows * chans * cols, transcendentals=0),
    )(*pieces, kernel)


def chan_swap(block, mask):
    size = lax.axis_size("chan")
    return lax.ppermute(block, "chan", [(i, i ^ mask) for i in range(size)])


def per_device(volume, kernel, cotangent):
    count, planes_in, rows_in, chans_in, cols_in = volume.shape
    planes_out = planes_in // 2
    rows_out = rows_in // 2
    cols_out = cols_in // 2
    chans_out = kernel.shape[2]
    groups = lax.axis_size("chan")
    share = chans_out // groups
    me = lax.axis_index("chan")
    kernel = jnp.concatenate(
        [lax.dynamic_slice_in_dim(kernel, (me ^ k) * share, share, axis=2) for k in range(groups)], axis=2
    )
    below = from_behind(volume[:, -1:], "space", 1)
    own_block, far_block, sent = forward_partial(below[0, 0], volume[0], kernel, groups)
    pair = jnp.concatenate([cotangent, from_behind(cotangent, "space", -1)], axis=1)[0]
    (own_block, far_block, sent), pair = lax.optimization_barrier(((own_block, far_block, sent), pair))
    near = chan_swap(sent, 1)
    across = chan_swap(pair, 2)
    far_sum = far_block + near[1]
    other = chan_swap(jnp.stack([pair, across]), 1)
    other, far_sum = lax.optimization_barrier((other, far_sum))
    total = (own_block + near[0]) + chan_swap(far_sum, 2)
    response = total.astype(jnp.bfloat16).reshape(count, planes_out, rows_out, share, cols_out)
    pieces = [pair, other[0], across, other[1]]
    volume_grad = backward_grad(pieces, kernel).reshape(count, planes_in, rows_in, chans_in, cols_in)
    return (response, volume_grad)


def solution(mesh):
    placed = (
        P("dp", "space", None, "chan", None),
        P(None, "chan", None),
        P("dp", "space", None, "chan", None),
    )
    return jax.shard_map(
        per_device,
        mesh=mesh,
        in_specs=placed,
        out_specs=(P("dp", "space", None, "chan", None), P("dp", "space", None, "chan", None)),
        check_vma=False,
    )
```

```python
import jax
import jax.numpy as jnp
from jax import lax
from jax.sharding import PartitionSpec as P
from jax.experimental import pallas as pl
from jax.experimental.pallas import tpu as pltpu


def from_behind(block, axis, distance):
    devices = range(lax.axis_size(axis))
    route = [(i - distance, i) for i in devices if i - distance in devices]
    return lax.ppermute(block, axis, route)


def shift_front(values, axis):
    widths = [(0, 0)] * values.ndim
    widths[axis] = (1, 0)
    return jnp.pad(lax.slice_in_dim(values, 0, values.shape[axis] - 1, 1, axis), widths)


def shift_back(values, axis):
    widths = [(0, 0)] * values.ndim
    widths[axis] = (0, 1)
    return jnp.pad(lax.slice_in_dim(values, 1, values.shape[axis], 1, axis), widths)


def transposed_phases(source, taps):
    shift_row = shift_back(source, 2)
    shift_col = shift_back(source, 4)
    shift_both = shift_back(shift_row, 4)
    sources = {(0, 0): source, (1, 0): shift_row, (0, 1): shift_col, (1, 1): shift_both}
    phases = {}
    for row_tap in range(3):
        for col_tap in range(3):
            picked = sources[int(row_tap == 0), int(col_tap == 0)]
            term = jnp.einsum(
                "bdhew,ce->bdhcw",
                picked,
                taps[row_tap, col_tap],
                preferred_element_type=jnp.float32,
            )
            place = (0 if row_tap == 1 else 1, 0 if col_tap == 1 else 1)
            phases[place] = term if place not in phases else phases[place] + term
    upper = jnp.stack([phases[0, 0], phases[0, 1]], axis=4)
    lower = jnp.stack([phases[1, 0], phases[1, 1]], axis=4)
    return jnp.stack([upper, lower], axis=3)


def spread_matrix(rows, cols, transposed):
    blocks = []
    for tap in range(3):
        narrow = lax.broadcasted_iota(jnp.int32, (rows, cols), 1 if not transposed else 0)
        wide = lax.broadcasted_iota(jnp.int32, (rows, cols), 0 if not transposed else 1)
        blocks.append(jnp.where(wide == 2 * narrow + tap - 1, 1.0, 0.0).astype(jnp.bfloat16))
    return jnp.concatenate(blocks, axis=1)


def forward_taps(source_refs, kbig_ref, acc_ref, out_refs, picked_ref, first_tap):
    planes = len(source_refs)
    rows, chans, cols = source_refs[0].shape
    rows_out, cols_out = rows // 2, cols // 2
    share = out_refs[0].shape[1]
    sel = spread_matrix(cols, cols_out, False)
    for plane, source_ref in enumerate(source_refs):
        flat = source_ref[...].reshape(rows * chans, cols)
        chosen = jnp.dot(flat, sel, preferred_element_type=jnp.float32)
        picked_ref[plane] = chosen.astype(picked_ref.dtype).reshape(rows, chans, 3 * cols_out)
    kpart = kbig_ref[:, first_tap * 9 * chans:(first_tap + planes) * 9 * chans]
    zero = jnp.zeros((chans, cols_out), picked_ref.dtype)
    for i in range(rows_out):
        pieces = []
        for plane in range(planes):
            for row_tap in range(3):
                row = 2 * i + row_tap - 1
                for col_tap in range(3):
                    if row < 0:
                        pieces.append(zero)
                    else:
                        pieces.append(picked_ref[plane, row, :, col_tap * cols_out:(col_tap + 1) * cols_out])
        stacked = jnp.concatenate(pieces, axis=0)
        result = jnp.dot(kpart, stacked, preferred_element_type=jnp.float32)
        if acc_ref is not None:
            result = acc_ref[i] + result
        if len(out_refs) == 1 and share == result.shape[0]:
            out_refs[0][i] = result
        else:
            for k, out_ref in enumerate(out_refs):
                out_ref[i] = result[k * share:(k + 1) * share]


def forward_local_rows(vol_ref, kbig_ref, acc_ref, picked_ref):
    forward_taps([vol_ref.at[0], vol_ref.at[1]], kbig_ref, None, [acc_ref], picked_ref, 1)


def forward_halo_rows(halo_ref, acc_ref, kbig_ref, *refs):
    out_refs, picked_ref = refs[:-1], refs[-1]
    forward_taps([halo_ref], kbig_ref, acc_ref, list(out_refs), picked_ref, 0)


def forward_partial(halo, vol, kernel, groups):
    planes, rows, chans, cols = vol.shape
    taps, _, chans_out = kernel.shape
    rows_out, cols_out = rows // 2, cols // 2
    share = chans_out // groups
    kbig = jnp.transpose(kernel, (2, 0, 1)).reshape(chans_out, taps * chans)
    vmem = pl.BlockSpec(memory_space=pltpu.VMEM)
    per_plane = 2 * rows * chans * cols * 3 * cols_out + 2 * rows_out * chans_out * 9 * chans * cols_out
    acc = pl.pallas_call(
        forward_local_rows,
        out_shape=jax.ShapeDtypeStruct((rows_out, chans_out, cols_out), jnp.float32),
        in_specs=[vmem] * 2,
        out_specs=vmem,
        scratch_shapes=[pltpu.VMEM((planes, rows, chans, 3 * cols_out), vol.dtype)],
        cost_estimate=pl.CostEstimate(flops=planes * per_plane, bytes_accessed=2 * vol.size + 4 * rows_out * chans_out * cols_out, transcendentals=0),
    )(vol, kbig)
    return pl.pallas_call(
        forward_halo_rows,
        out_shape=[jax.ShapeDtypeStruct((rows_out, share, cols_out), jnp.float32)] * groups,
        in_specs=[vmem] * 3,
        out_specs=[vmem] * groups,
        scratch_shapes=[pltpu.VMEM((1, rows, chans, 3 * cols_out), vol.dtype)],
        cost_estimate=pl.CostEstimate(flops=per_plane, bytes_accessed=2 * halo.size + 8 * rows_out * chans_out * cols_out, transcendentals=0),
    )(halo, acc, kbig)


def backward_rows(*refs):
    groups = (len(refs) - 3)
    cot_refs, k_ref, out_ref, up_ref = refs[:groups], refs[groups], refs[groups + 1], refs[groups + 2]
    planes, rows_out, share, cols_out = cot_refs[0].shape
    rows = out_ref.shape[1]
    cols = out_ref.shape[3]
    tsel = spread_matrix(cols_out, cols, True)
    for k, cot_ref in enumerate(cot_refs):
        flat = cot_ref[...].reshape(planes * rows_out * share, cols_out)
        spread = jnp.dot(flat, tsel, preferred_element_type=jnp.float32)
        up_ref[:, :, k * share:(k + 1) * share, :] = spread.astype(up_ref.dtype).reshape(planes, rows_out, share, 3 * cols)
    for depth in range(2):
        sources = [(1, 0)] if depth == 0 else [(2, 0), (0, 1)]
        for row in range(rows):
            weights, values = [], []
            for depth_tap, plane in sources:
                for row_tap in range(3):
                    if (row + 1 - row_tap) % 2:
                        continue
                    i = (row + 1 - row_tap) // 2
                    if not 0 <= i < rows_out:
                        continue
                    for col_tap in range(3):
                        weights.append(k_ref[9 * depth_tap + 3 * row_tap + col_tap])
                        values.append(up_ref[plane, i, :, col_tap * cols:(col_tap + 1) * cols])
            lhs = jnp.concatenate(weights, axis=1)
            rhs = jnp.concatenate(values, axis=0)
            out_ref[depth, row] = jnp.dot(lhs, rhs, preferred_element_type=jnp.float32).astype(out_ref.dtype)


def backward_grad(pieces, kernel):
    planes, rows_out, share, cols_out = pieces[0].shape
    chans_out = share * len(pieces)
    taps, chans, _ = kernel.shape
    rows, cols = 2 * rows_out, 2 * cols_out
    flops = 2 * planes * rows_out * chans_out * cols_out * 3 * cols + 2 * 2 * rows * chans * 9 * chans_out * cols
    return pl.pallas_call(
        backward_rows,
        out_shape=jax.ShapeDtypeStruct((2, rows, chans, cols), kernel.dtype),
        in_specs=[pl.BlockSpec(memory_space=pltpu.VMEM)] * (len(pieces) + 1),
        out_specs=pl.BlockSpec(memory_space=pltpu.VMEM),
        scratch_shapes=[pltpu.VMEM((planes, rows_out, chans_out, 3 * cols), kernel.dtype)],
        cost_estimate=pl.CostEstimate(flops=flops, bytes_accessed=2 * planes * rows_out * chans_out * cols_out + 2 * 2 * rows * chans * cols, transcendentals=0),
    )(*pieces, kernel)


def chan_shift(block, shift):
    size = lax.axis_size("chan")
    return lax.ppermute(block, "chan", [(i, (i + shift) % size) for i in range(size)])


def per_device(volume, kernel, cotangent):
    count, planes_in, rows_in, chans_in, cols_in = volume.shape
    planes_out = planes_in // 2
    rows_out = rows_in // 2
    cols_out = cols_in // 2
    chans_out = kernel.shape[2]
    groups = lax.axis_size("chan")
    share = chans_out // groups
    me = lax.axis_index("chan")
    kernel = jnp.roll(kernel, -me * share, axis=2)
    below = from_behind(volume[:, -1:], "space", 1)
    pair = jnp.concatenate([cotangent, from_behind(cotangent, "space", -1)], axis=1)
    pieces = [pair[0]] + [chan_shift(pair[0], -k) for k in range(1, groups)]
    pieces, below = lax.optimization_barrier((pieces, below))
    chunks = forward_partial(below[0, 0], volume[0], kernel, groups)
    total = chunks[0]
    for k in range(1, groups):
        total = total + chan_shift(chunks[k], k)
    response = total.astype(jnp.bfloat16).reshape(count, planes_out, rows_out, share, cols_out)
    volume_grad = backward_grad(pieces, kernel).reshape(count, planes_in, rows_in, chans_in, cols_in)
    return (response, volume_grad)


def solution(mesh):
    placed = (
        P("dp", "space", None, "chan", None),
        P(None, "chan", None),
        P("dp", "space", None, "chan", None),
    )
    return jax.shard_map(
        per_device,
        mesh=mesh,
        in_specs=placed,
        out_specs=(P("dp", "space", None, "chan", None), P("dp", "space", None, "chan", None)),
        check_vma=False,
    )
```

```python
import jax
import jax.numpy as jnp
from jax import lax
from jax.sharding import PartitionSpec as P
from jax.experimental import pallas as pl
from jax.experimental.pallas import tpu as pltpu


def from_behind(block, axis, distance):
    devices = range(lax.axis_size(axis))
    route = [(i - distance, i) for i in devices if i - distance in devices]
    return lax.ppermute(block, axis, route)


def shift_front(values, axis):
    widths = [(0, 0)] * values.ndim
    widths[axis] = (1, 0)
    return jnp.pad(lax.slice_in_dim(values, 0, values.shape[axis] - 1, 1, axis), widths)


def shift_back(values, axis):
    widths = [(0, 0)] * values.ndim
    widths[axis] = (0, 1)
    return jnp.pad(lax.slice_in_dim(values, 1, values.shape[axis], 1, axis), widths)


def transposed_phases(source, taps):
    shift_row = shift_back(source, 2)
    shift_col = shift_back(source, 4)
    shift_both = shift_back(shift_row, 4)
    sources = {(0, 0): source, (1, 0): shift_row, (0, 1): shift_col, (1, 1): shift_both}
    phases = {}
    for row_tap in range(3):
        for col_tap in range(3):
            picked = sources[int(row_tap == 0), int(col_tap == 0)]
            term = jnp.einsum(
                "bdhew,ce->bdhcw",
                picked,
                taps[row_tap, col_tap],
                preferred_element_type=jnp.float32,
            )
            place = (0 if row_tap == 1 else 1, 0 if col_tap == 1 else 1)
            phases[place] = term if place not in phases else phases[place] + term
    upper = jnp.stack([phases[0, 0], phases[0, 1]], axis=4)
    lower = jnp.stack([phases[1, 0], phases[1, 1]], axis=4)
    return jnp.stack([upper, lower], axis=3)


def spread_matrix(rows, cols, transposed):
    blocks = []
    for tap in range(3):
        narrow = lax.broadcasted_iota(jnp.int32, (rows, cols), 1 if not transposed else 0)
        wide = lax.broadcasted_iota(jnp.int32, (rows, cols), 0 if not transposed else 1)
        blocks.append(jnp.where(wide == 2 * narrow + tap - 1, 1.0, 0.0).astype(jnp.bfloat16))
    return jnp.concatenate(blocks, axis=1)


def forward_taps(source_refs, kbig_ref, acc_ref, out_refs, picked_ref):
    planes = len(source_refs)
    rows, chans, cols = source_refs[0].shape
    rows_out, cols_out = rows // 2, cols // 2
    share = out_refs[0].shape[1]
    sel = spread_matrix(cols, cols_out, False)
    for plane, source_ref in enumerate(source_refs):
        flat = source_ref[...].reshape(rows * chans, cols)
        chosen = jnp.dot(flat, sel, preferred_element_type=jnp.float32)
        picked_ref[plane] = chosen.astype(picked_ref.dtype).reshape(rows, chans, 3 * cols_out)
    kpart = kbig_ref[...]
    zero = jnp.zeros((chans, cols_out), picked_ref.dtype)
    for i in range(rows_out):
        pieces = []
        for plane in range(planes):
            for row_tap in range(3):
                row = 2 * i + row_tap - 1
                for col_tap in range(3):
                    if row < 0:
                        pieces.append(zero)
                    else:
                        pieces.append(picked_ref[plane, row, :, col_tap * cols_out:(col_tap + 1) * cols_out])
        stacked = jnp.concatenate(pieces, axis=0)
        result = jnp.dot(kpart, stacked, preferred_element_type=jnp.float32)
        if acc_ref is not None:
            result = acc_ref[i] + result
        if len(out_refs) == 1 and share == result.shape[0]:
            out_refs[0][i] = result
        else:
            for k, out_ref in enumerate(out_refs):
                out_ref[i] = result[k * share:(k + 1) * share]


def forward_local_rows(vol_ref, kbig_ref, acc_ref, picked_ref):
    forward_taps([vol_ref.at[0], vol_ref.at[1]], kbig_ref, None, [acc_ref], picked_ref)


def forward_halo_rows(halo_ref, acc_ref, kbig_ref, *refs):
    out_refs, picked_ref = refs[:-1], refs[-1]
    forward_taps([halo_ref], kbig_ref, acc_ref, list(out_refs), picked_ref)


def forward_partial(halo, vol, kernel, groups):
    planes, rows, chans, cols = vol.shape
    taps, _, chans_out = kernel.shape
    rows_out, cols_out = rows // 2, cols // 2
    share = chans_out // groups
    kbig = jnp.transpose(kernel, (2, 0, 1)).reshape(chans_out, taps * chans)
    vmem = pl.BlockSpec(memory_space=pltpu.VMEM)
    per_plane = 2 * rows * chans * cols * 3 * cols_out + 2 * rows_out * chans_out * 9 * chans * cols_out
    acc = pl.pallas_call(
        forward_local_rows,
        out_shape=jax.ShapeDtypeStruct((rows_out, chans_out, cols_out), jnp.float32),
        in_specs=[vmem] * 2,
        out_specs=vmem,
        scratch_shapes=[pltpu.VMEM((planes, rows, chans, 3 * cols_out), vol.dtype)],
        cost_estimate=pl.CostEstimate(flops=planes * per_plane, bytes_accessed=2 * vol.size + 4 * rows_out * chans_out * cols_out, transcendentals=0),
    )(vol, kbig[:, 9 * chans:])
    return pl.pallas_call(
        forward_halo_rows,
        out_shape=[jax.ShapeDtypeStruct((rows_out, share, cols_out), jnp.float32)] * groups,
        in_specs=[vmem] * 3,
        out_specs=[vmem] * groups,
        scratch_shapes=[pltpu.VMEM((1, rows, chans, 3 * cols_out), vol.dtype)],
        cost_estimate=pl.CostEstimate(flops=per_plane, bytes_accessed=2 * halo.size + 8 * rows_out * chans_out * cols_out, transcendentals=0),
    )(halo, acc, kbig[:, :9 * chans])


def backward_rows(*refs):
    groups = (len(refs) - 3)
    cot_refs, k_ref, out_ref, up_ref = refs[:groups], refs[groups], refs[groups + 1], refs[groups + 2]
    planes, rows_out, share, cols_out = cot_refs[0].shape
    rows = out_ref.shape[1]
    cols = out_ref.shape[3]
    tsel = spread_matrix(cols_out, cols, True)
    for k, cot_ref in enumerate(cot_refs):
        flat = cot_ref[...].reshape(planes * rows_out * share, cols_out)
        spread = jnp.dot(flat, tsel, preferred_element_type=jnp.float32)
        up_ref[:, :, k * share:(k + 1) * share, :] = spread.astype(up_ref.dtype).reshape(planes, rows_out, share, 3 * cols)
    for depth in range(2):
        sources = [(1, 0)] if depth == 0 else [(2, 0), (0, 1)]
        for row in range(rows):
            weights, values = [], []
            for depth_tap, plane in sources:
                for row_tap in range(3):
                    if (row + 1 - row_tap) % 2:
                        continue
                    i = (row + 1 - row_tap) // 2
                    if not 0 <= i < rows_out:
                        continue
                    for col_tap in range(3):
                        weights.append(k_ref[9 * depth_tap + 3 * row_tap + col_tap])
                        values.append(up_ref[plane, i, :, col_tap * cols:(col_tap + 1) * cols])
            lhs = jnp.concatenate(weights, axis=1)
            rhs = jnp.concatenate(values, axis=0)
            out_ref[depth, row] = jnp.dot(lhs, rhs, preferred_element_type=jnp.float32).astype(out_ref.dtype)


def backward_grad(pieces, kernel):
    planes, rows_out, share, cols_out = pieces[0].shape
    chans_out = share * len(pieces)
    taps, chans, _ = kernel.shape
    rows, cols = 2 * rows_out, 2 * cols_out
    flops = 2 * planes * rows_out * chans_out * cols_out * 3 * cols + 2 * 2 * rows * chans * 9 * chans_out * cols
    return pl.pallas_call(
        backward_rows,
        out_shape=jax.ShapeDtypeStruct((2, rows, chans, cols), kernel.dtype),
        in_specs=[pl.BlockSpec(memory_space=pltpu.VMEM)] * (len(pieces) + 1),
        out_specs=pl.BlockSpec(memory_space=pltpu.VMEM),
        scratch_shapes=[pltpu.VMEM((planes, rows_out, chans_out, 3 * cols), kernel.dtype)],
        cost_estimate=pl.CostEstimate(flops=flops, bytes_accessed=2 * planes * rows_out * chans_out * cols_out + 2 * 2 * rows * chans * cols, transcendentals=0),
    )(*pieces, kernel)


def chan_shift(block, shift):
    size = lax.axis_size("chan")
    return lax.ppermute(block, "chan", [(i, (i + shift) % size) for i in range(size)])


def per_device(volume, kernel, cotangent):
    count, planes_in, rows_in, chans_in, cols_in = volume.shape
    planes_out = planes_in // 2
    rows_out = rows_in // 2
    cols_out = cols_in // 2
    chans_out = kernel.shape[2]
    groups = lax.axis_size("chan")
    share = chans_out // groups
    me = lax.axis_index("chan")
    kernel = jnp.roll(kernel, -me * share, axis=2)
    below = from_behind(volume[:, -1:], "space", 1)
    chunks = forward_partial(below[0, 0], volume[0], kernel, groups)
    pair = jnp.concatenate([cotangent, from_behind(cotangent, "space", -1)], axis=1)
    chunks, pair = lax.optimization_barrier((chunks, pair))
    total = chunks[0]
    for k in range(1, groups):
        total = total + chan_shift(chunks[k], k)
    response = total.astype(jnp.bfloat16).reshape(count, planes_out, rows_out, share, cols_out)
    pieces = [pair[0]] + [chan_shift(pair[0], -k) for k in range(1, groups)]
    volume_grad = backward_grad(pieces, kernel).reshape(count, planes_in, rows_in, chans_in, cols_in)
    return (response, volume_grad)


def solution(mesh):
    placed = (
        P("dp", "space", None, "chan", None),
        P(None, "chan", None),
        P("dp", "space", None, "chan", None),
    )
    return jax.shard_map(
        per_device,
        mesh=mesh,
        in_specs=placed,
        out_specs=(P("dp", "space", None, "chan", None), P("dp", "space", None, "chan", None)),
        check_vma=False,
    )
```

```python
import jax
import jax.numpy as jnp
from jax import lax
from jax.sharding import PartitionSpec as P
from jax.experimental import pallas as pl
from jax.experimental.pallas import tpu as pltpu


def from_behind(block, axis, distance):
    devices = range(lax.axis_size(axis))
    route = [(i - distance, i) for i in devices if i - distance in devices]
    return lax.ppermute(block, axis, route)


def shift_front(values, axis):
    widths = [(0, 0)] * values.ndim
    widths[axis] = (1, 0)
    return jnp.pad(lax.slice_in_dim(values, 0, values.shape[axis] - 1, 1, axis), widths)


def shift_back(values, axis):
    widths = [(0, 0)] * values.ndim
    widths[axis] = (0, 1)
    return jnp.pad(lax.slice_in_dim(values, 1, values.shape[axis], 1, axis), widths)


def transposed_phases(source, taps):
    shift_row = shift_back(source, 2)
    shift_col = shift_back(source, 4)
    shift_both = shift_back(shift_row, 4)
    sources = {(0, 0): source, (1, 0): shift_row, (0, 1): shift_col, (1, 1): shift_both}
    phases = {}
    for row_tap in range(3):
        for col_tap in range(3):
            picked = sources[int(row_tap == 0), int(col_tap == 0)]
            term = jnp.einsum(
                "bdhew,ce->bdhcw",
                picked,
                taps[row_tap, col_tap],
                preferred_element_type=jnp.float32,
            )
            place = (0 if row_tap == 1 else 1, 0 if col_tap == 1 else 1)
            phases[place] = term if place not in phases else phases[place] + term
    upper = jnp.stack([phases[0, 0], phases[0, 1]], axis=4)
    lower = jnp.stack([phases[1, 0], phases[1, 1]], axis=4)
    return jnp.stack([upper, lower], axis=3)


def spread_matrix(rows, cols, transposed):
    blocks = []
    for tap in range(3):
        narrow = lax.broadcasted_iota(jnp.int32, (rows, cols), 1 if not transposed else 0)
        wide = lax.broadcasted_iota(jnp.int32, (rows, cols), 0 if not transposed else 1)
        blocks.append(jnp.where(wide == 2 * narrow + tap - 1, 1.0, 0.0).astype(jnp.bfloat16))
    return jnp.concatenate(blocks, axis=1)


def forward_taps(source_refs, kbig_ref, acc_ref, out_refs, picked_ref, first_tap):
    planes = len(source_refs)
    rows, chans, cols = source_refs[0].shape
    rows_out, cols_out = rows // 2, cols // 2
    share = out_refs[0].shape[1]
    sel = spread_matrix(cols, cols_out, False)
    for plane, source_ref in enumerate(source_refs):
        flat = source_ref[...].reshape(rows * chans, cols)
        chosen = jnp.dot(flat, sel, preferred_element_type=jnp.float32)
        picked_ref[plane] = chosen.astype(picked_ref.dtype).reshape(rows, chans, 3 * cols_out)
    kpart = kbig_ref[:, first_tap * 9 * chans:(first_tap + planes) * 9 * chans]
    zero = jnp.zeros((chans, cols_out), picked_ref.dtype)
    for i in range(rows_out):
        pieces = []
        for plane in range(planes):
            for row_tap in range(3):
                row = 2 * i + row_tap - 1
                for col_tap in range(3):
                    if row < 0:
                        pieces.append(zero)
                    else:
                        pieces.append(picked_ref[plane, row, :, col_tap * cols_out:(col_tap + 1) * cols_out])
        stacked = jnp.concatenate(pieces, axis=0)
        result = jnp.dot(kpart, stacked, preferred_element_type=jnp.float32)
        if acc_ref is not None:
            result = acc_ref[i] + result
        if len(out_refs) == 1 and share == result.shape[0]:
            out_refs[0][i] = result
        else:
            for k, out_ref in enumerate(out_refs):
                out_ref[i] = result[k * share:(k + 1) * share]


def forward_local_rows(vol_ref, kbig_ref, acc_ref, picked_ref):
    forward_taps([vol_ref.at[0], vol_ref.at[1]], kbig_ref, None, [acc_ref], picked_ref, 1)


def forward_halo_rows(halo_ref, acc_ref, kbig_ref, *refs):
    out_refs, picked_ref = refs[:-1], refs[-1]
    forward_taps([halo_ref], kbig_ref, acc_ref, list(out_refs), picked_ref, 0)


def forward_partial(halo, vol, kernel, groups):
    planes, rows, chans, cols = vol.shape
    taps, _, chans_out = kernel.shape
    rows_out, cols_out = rows // 2, cols // 2
    share = chans_out // groups
    kbig = jnp.transpose(kernel, (2, 0, 1)).reshape(chans_out, taps * chans)
    vmem = pl.BlockSpec(memory_space=pltpu.VMEM)
    per_plane = 2 * rows * chans * cols * 3 * cols_out + 2 * rows_out * chans_out * 9 * chans * cols_out
    acc = pl.pallas_call(
        forward_local_rows,
        out_shape=jax.ShapeDtypeStruct((rows_out, chans_out, cols_out), jnp.float32),
        in_specs=[vmem] * 2,
        out_specs=vmem,
        scratch_shapes=[pltpu.VMEM((planes, rows, chans, 3 * cols_out), vol.dtype)],
        cost_estimate=pl.CostEstimate(flops=planes * per_plane, bytes_accessed=2 * vol.size + 4 * rows_out * chans_out * cols_out, transcendentals=0),
    )(vol, kbig)
    return pl.pallas_call(
        forward_halo_rows,
        out_shape=[jax.ShapeDtypeStruct((rows_out, share, cols_out), jnp.float32)] * groups,
        in_specs=[vmem] * 3,
        out_specs=[vmem] * groups,
        scratch_shapes=[pltpu.VMEM((1, rows, chans, 3 * cols_out), vol.dtype)],
        cost_estimate=pl.CostEstimate(flops=per_plane, bytes_accessed=2 * halo.size + 8 * rows_out * chans_out * cols_out, transcendentals=0),
    )(pltpu.with_memory_space_constraint(halo, pltpu.MemorySpace.VMEM), acc, kbig)


def backward_rows(*refs):
    groups = (len(refs) - 3)
    cot_refs, k_ref, out_ref, up_ref = refs[:groups], refs[groups], refs[groups + 1], refs[groups + 2]
    planes, rows_out, share, cols_out = cot_refs[0].shape
    rows = out_ref.shape[1]
    cols = out_ref.shape[3]
    tsel = spread_matrix(cols_out, cols, True)
    for k, cot_ref in enumerate(cot_refs):
        flat = cot_ref[...].reshape(planes * rows_out * share, cols_out)
        spread = jnp.dot(flat, tsel, preferred_element_type=jnp.float32)
        up_ref[:, :, k * share:(k + 1) * share, :] = spread.astype(up_ref.dtype).reshape(planes, rows_out, share, 3 * cols)
    for depth in range(2):
        sources = [(1, 0)] if depth == 0 else [(2, 0), (0, 1)]
        for row in range(rows):
            weights, values = [], []
            for depth_tap, plane in sources:
                for row_tap in range(3):
                    if (row + 1 - row_tap) % 2:
                        continue
                    i = (row + 1 - row_tap) // 2
                    if not 0 <= i < rows_out:
                        continue
                    for col_tap in range(3):
                        weights.append(k_ref[9 * depth_tap + 3 * row_tap + col_tap])
                        values.append(up_ref[plane, i, :, col_tap * cols:(col_tap + 1) * cols])
            lhs = jnp.concatenate(weights, axis=1)
            rhs = jnp.concatenate(values, axis=0)
            out_ref[depth, row] = jnp.dot(lhs, rhs, preferred_element_type=jnp.float32).astype(out_ref.dtype)


def backward_grad(pieces, kernel):
    planes, rows_out, share, cols_out = pieces[0].shape
    chans_out = share * len(pieces)
    taps, chans, _ = kernel.shape
    rows, cols = 2 * rows_out, 2 * cols_out
    flops = 2 * planes * rows_out * chans_out * cols_out * 3 * cols + 2 * 2 * rows * chans * 9 * chans_out * cols
    return pl.pallas_call(
        backward_rows,
        out_shape=jax.ShapeDtypeStruct((2, rows, chans, cols), kernel.dtype),
        in_specs=[pl.BlockSpec(memory_space=pltpu.VMEM)] * (len(pieces) + 1),
        out_specs=pl.BlockSpec(memory_space=pltpu.VMEM),
        scratch_shapes=[pltpu.VMEM((planes, rows_out, chans_out, 3 * cols), kernel.dtype)],
        cost_estimate=pl.CostEstimate(flops=flops, bytes_accessed=2 * planes * rows_out * chans_out * cols_out + 2 * 2 * rows * chans * cols, transcendentals=0),
    )(*pieces, kernel)


def chan_shift(block, shift):
    size = lax.axis_size("chan")
    return lax.ppermute(block, "chan", [(i, (i + shift) % size) for i in range(size)])


def per_device(volume, kernel, cotangent):
    count, planes_in, rows_in, chans_in, cols_in = volume.shape
    planes_out = planes_in // 2
    rows_out = rows_in // 2
    cols_out = cols_in // 2
    chans_out = kernel.shape[2]
    groups = lax.axis_size("chan")
    share = chans_out // groups
    me = lax.axis_index("chan")
    kernel = jnp.roll(kernel, -me * share, axis=2)
    below = from_behind(volume[:, -1:], "space", 1)
    chunks = forward_partial(below[0, 0], volume[0], kernel, groups)
    pair = jnp.concatenate([cotangent, from_behind(cotangent, "space", -1)], axis=1)
    chunks, pair = lax.optimization_barrier((chunks, pair))
    total = chunks[0]
    for k in range(1, groups):
        total = total + chan_shift(chunks[k], k)
    response = total.astype(jnp.bfloat16).reshape(count, planes_out, rows_out, share, cols_out)
    pieces = [pair[0]] + [chan_shift(pair[0], -k) for k in range(1, groups)]
    volume_grad = backward_grad(pieces, kernel).reshape(count, planes_in, rows_in, chans_in, cols_in)
    return (response, volume_grad)


def solution(mesh):
    placed = (
        P("dp", "space", None, "chan", None),
        P(None, "chan", None),
        P("dp", "space", None, "chan", None),
    )
    return jax.shard_map(
        per_device,
        mesh=mesh,
        in_specs=placed,
        out_specs=(P("dp", "space", None, "chan", None), P("dp", "space", None, "chan", None)),
        check_vma=False,
    )
```

```python
import jax
import jax.numpy as jnp
from jax import lax
from jax.sharding import PartitionSpec as P
from jax.experimental import pallas as pl
from jax.experimental.pallas import tpu as pltpu


def from_behind(block, axis, distance):
    devices = range(lax.axis_size(axis))
    route = [(i - distance, i) for i in devices if i - distance in devices]
    return lax.ppermute(block, axis, route)


def shift_front(values, axis):
    widths = [(0, 0)] * values.ndim
    widths[axis] = (1, 0)
    return jnp.pad(lax.slice_in_dim(values, 0, values.shape[axis] - 1, 1, axis), widths)


def shift_back(values, axis):
    widths = [(0, 0)] * values.ndim
    widths[axis] = (0, 1)
    return jnp.pad(lax.slice_in_dim(values, 1, values.shape[axis], 1, axis), widths)


def transposed_phases(source, taps):
    shift_row = shift_back(source, 2)
    shift_col = shift_back(source, 4)
    shift_both = shift_back(shift_row, 4)
    sources = {(0, 0): source, (1, 0): shift_row, (0, 1): shift_col, (1, 1): shift_both}
    phases = {}
    for row_tap in range(3):
        for col_tap in range(3):
            picked = sources[int(row_tap == 0), int(col_tap == 0)]
            term = jnp.einsum(
                "bdhew,ce->bdhcw",
                picked,
                taps[row_tap, col_tap],
                preferred_element_type=jnp.float32,
            )
            place = (0 if row_tap == 1 else 1, 0 if col_tap == 1 else 1)
            phases[place] = term if place not in phases else phases[place] + term
    upper = jnp.stack([phases[0, 0], phases[0, 1]], axis=4)
    lower = jnp.stack([phases[1, 0], phases[1, 1]], axis=4)
    return jnp.stack([upper, lower], axis=3)


def spread_matrix(rows, cols, transposed):
    blocks = []
    for tap in range(3):
        narrow = lax.broadcasted_iota(jnp.int32, (rows, cols), 1 if not transposed else 0)
        wide = lax.broadcasted_iota(jnp.int32, (rows, cols), 0 if not transposed else 1)
        blocks.append(jnp.where(wide == 2 * narrow + tap - 1, 1.0, 0.0).astype(jnp.bfloat16))
    return jnp.concatenate(blocks, axis=1)


def forward_taps(source_refs, kbig_ref, acc_ref, out_refs, picked_ref, first_tap):
    planes = len(source_refs)
    rows, chans, cols = source_refs[0].shape
    rows_out, cols_out = rows // 2, cols // 2
    share = out_refs[0].shape[1]
    sel = spread_matrix(cols, cols_out, False)
    for plane, source_ref in enumerate(source_refs):
        flat = source_ref[...].reshape(rows * chans, cols)
        chosen = jnp.dot(flat, sel, preferred_element_type=jnp.float32)
        picked_ref[plane] = chosen.astype(picked_ref.dtype).reshape(rows, chans, 3 * cols_out)
    kpart = kbig_ref[:, first_tap * 9 * chans:(first_tap + planes) * 9 * chans]
    zero = jnp.zeros((chans, cols_out), picked_ref.dtype)
    for i in range(rows_out):
        pieces = []
        for plane in range(planes):
            for row_tap in range(3):
                row = 2 * i + row_tap - 1
                for col_tap in range(3):
                    if row < 0:
                        pieces.append(zero)
                    else:
                        pieces.append(picked_ref[plane, row, :, col_tap * cols_out:(col_tap + 1) * cols_out])
        stacked = jnp.concatenate(pieces, axis=0)
        result = jnp.dot(kpart, stacked, preferred_element_type=jnp.float32)
        if acc_ref is not None:
            result = acc_ref[i] + result
        if len(out_refs) == 1 and share == result.shape[0]:
            out_refs[0][i] = result
        else:
            for k, out_ref in enumerate(out_refs):
                out_ref[i] = result[k * share:(k + 1) * share]


def forward_local_rows(vol_ref, kbig_ref, acc_ref, picked_ref):
    forward_taps([vol_ref.at[0], vol_ref.at[1]], kbig_ref, None, [acc_ref], picked_ref, 1)


def forward_halo_rows(halo_ref, acc_ref, kbig_ref, *refs):
    out_refs, picked_ref = refs[:-1], refs[-1]
    forward_taps([halo_ref], kbig_ref, acc_ref, list(out_refs), picked_ref, 0)


def forward_partial(halo, vol, kernel, groups):
    planes, rows, chans, cols = vol.shape
    taps, _, chans_out = kernel.shape
    rows_out, cols_out = rows // 2, cols // 2
    share = chans_out // groups
    kbig = jnp.transpose(kernel, (2, 0, 1)).reshape(chans_out, taps * chans)
    vmem = pl.BlockSpec(memory_space=pltpu.VMEM)
    per_plane = 2 * rows * chans * cols * 3 * cols_out + 2 * rows_out * chans_out * 9 * chans * cols_out
    acc = pl.pallas_call(
        forward_local_rows,
        out_shape=jax.ShapeDtypeStruct((rows_out, chans_out, cols_out), jnp.float32),
        in_specs=[vmem] * 2,
        out_specs=vmem,
        scratch_shapes=[pltpu.VMEM((planes, rows, chans, 3 * cols_out), vol.dtype)],
        cost_estimate=pl.CostEstimate(flops=planes * per_plane, bytes_accessed=2 * vol.size + 4 * rows_out * chans_out * cols_out, transcendentals=0),
    )(vol, kbig)
    return pl.pallas_call(
        forward_halo_rows,
        out_shape=[jax.ShapeDtypeStruct((rows_out, share, cols_out), jnp.float32)] * groups,
        in_specs=[vmem] * 3,
        out_specs=[vmem] * groups,
        scratch_shapes=[pltpu.VMEM((1, rows, chans, 3 * cols_out), vol.dtype)],
        cost_estimate=pl.CostEstimate(flops=per_plane, bytes_accessed=2 * halo.size + 8 * rows_out * chans_out * cols_out, transcendentals=0),
    )(pltpu.with_memory_space_constraint(halo, pltpu.MemorySpace.VMEM), acc, kbig)


def backward_rows(*refs):
    groups = (len(refs) - 3)
    cot_refs, k_ref, out_ref, up_ref = refs[:groups], refs[groups], refs[groups + 1], refs[groups + 2]
    planes, rows_out, share, cols_out = cot_refs[0].shape
    rows = out_ref.shape[1]
    cols = out_ref.shape[3]
    tsel = spread_matrix(cols_out, cols, True)
    for k, cot_ref in enumerate(cot_refs):
        flat = cot_ref[...].reshape(planes * rows_out * share, cols_out)
        spread = jnp.dot(flat, tsel, preferred_element_type=jnp.float32)
        up_ref[:, :, k * share:(k + 1) * share, :] = spread.astype(up_ref.dtype).reshape(planes, rows_out, share, 3 * cols)
    for depth in range(2):
        sources = [(1, 0)] if depth == 0 else [(2, 0), (0, 1)]
        for row in range(rows):
            weights, values = [], []
            for depth_tap, plane in sources:
                for row_tap in range(3):
                    if (row + 1 - row_tap) % 2:
                        continue
                    i = (row + 1 - row_tap) // 2
                    if not 0 <= i < rows_out:
                        continue
                    for col_tap in range(3):
                        weights.append(k_ref[9 * depth_tap + 3 * row_tap + col_tap])
                        values.append(up_ref[plane, i, :, col_tap * cols:(col_tap + 1) * cols])
            lhs = jnp.concatenate(weights, axis=1)
            rhs = jnp.concatenate(values, axis=0)
            out_ref[depth, row] = jnp.dot(lhs, rhs, preferred_element_type=jnp.float32).astype(out_ref.dtype)


def backward_grad(pieces, kernel):
    planes, rows_out, share, cols_out = pieces[0].shape
    chans_out = share * len(pieces)
    taps, chans, _ = kernel.shape
    rows, cols = 2 * rows_out, 2 * cols_out
    flops = 2 * planes * rows_out * chans_out * cols_out * 3 * cols + 2 * 2 * rows * chans * 9 * chans_out * cols
    return pl.pallas_call(
        backward_rows,
        out_shape=jax.ShapeDtypeStruct((2, rows, chans, cols), kernel.dtype),
        in_specs=[pl.BlockSpec(memory_space=pltpu.VMEM)] * (len(pieces) + 1),
        out_specs=pl.BlockSpec(memory_space=pltpu.VMEM),
        scratch_shapes=[pltpu.VMEM((planes, rows_out, chans_out, 3 * cols), kernel.dtype)],
        cost_estimate=pl.CostEstimate(flops=flops, bytes_accessed=2 * planes * rows_out * chans_out * cols_out + 2 * 2 * rows * chans * cols, transcendentals=0),
    )(*[pltpu.with_memory_space_constraint(piece, pltpu.MemorySpace.VMEM) for piece in pieces], kernel)


def chan_shift(block, shift):
    size = lax.axis_size("chan")
    return lax.ppermute(block, "chan", [(i, (i + shift) % size) for i in range(size)])


def per_device(volume, kernel, cotangent):
    count, planes_in, rows_in, chans_in, cols_in = volume.shape
    planes_out = planes_in // 2
    rows_out = rows_in // 2
    cols_out = cols_in // 2
    chans_out = kernel.shape[2]
    groups = lax.axis_size("chan")
    share = chans_out // groups
    me = lax.axis_index("chan")
    kernel = jnp.roll(kernel, -me * share, axis=2)
    below = from_behind(volume[:, -1:], "space", 1)
    chunks = forward_partial(below[0, 0], volume[0], kernel, groups)
    pair = jnp.concatenate([cotangent, from_behind(cotangent, "space", -1)], axis=1)
    chunks, pair = lax.optimization_barrier((chunks, pair))
    total = chunks[0]
    for k in range(1, groups):
        total = total + chan_shift(chunks[k], k)
    response = total.astype(jnp.bfloat16).reshape(count, planes_out, rows_out, share, cols_out)
    pieces = [pair[0]] + [chan_shift(pair[0], -k) for k in range(1, groups)]
    volume_grad = backward_grad(pieces, kernel).reshape(count, planes_in, rows_in, chans_in, cols_in)
    return (response, volume_grad)


def solution(mesh):
    placed = (
        P("dp", "space", None, "chan", None),
        P(None, "chan", None),
        P("dp", "space", None, "chan", None),
    )
    return jax.shard_map(
        per_device,
        mesh=mesh,
        in_specs=placed,
        out_specs=(P("dp", "space", None, "chan", None), P("dp", "space", None, "chan", None)),
        check_vma=False,
    )
```

```python
import jax
import jax.numpy as jnp
from jax import lax
from jax.sharding import PartitionSpec as P
from jax.experimental import pallas as pl
from jax.experimental.pallas import tpu as pltpu


def from_behind(block, axis, distance):
    devices = range(lax.axis_size(axis))
    route = [(i - distance, i) for i in devices if i - distance in devices]
    return lax.ppermute(block, axis, route)


def shift_front(values, axis):
    widths = [(0, 0)] * values.ndim
    widths[axis] = (1, 0)
    return jnp.pad(lax.slice_in_dim(values, 0, values.shape[axis] - 1, 1, axis), widths)


def shift_back(values, axis):
    widths = [(0, 0)] * values.ndim
    widths[axis] = (0, 1)
    return jnp.pad(lax.slice_in_dim(values, 1, values.shape[axis], 1, axis), widths)


def transposed_phases(source, taps):
    shift_row = shift_back(source, 2)
    shift_col = shift_back(source, 4)
    shift_both = shift_back(shift_row, 4)
    sources = {(0, 0): source, (1, 0): shift_row, (0, 1): shift_col, (1, 1): shift_both}
    phases = {}
    for row_tap in range(3):
        for col_tap in range(3):
            picked = sources[int(row_tap == 0), int(col_tap == 0)]
            term = jnp.einsum(
                "bdhew,ce->bdhcw",
                picked,
                taps[row_tap, col_tap],
                preferred_element_type=jnp.float32,
            )
            place = (0 if row_tap == 1 else 1, 0 if col_tap == 1 else 1)
            phases[place] = term if place not in phases else phases[place] + term
    upper = jnp.stack([phases[0, 0], phases[0, 1]], axis=4)
    lower = jnp.stack([phases[1, 0], phases[1, 1]], axis=4)
    return jnp.stack([upper, lower], axis=3)


def spread_matrix(rows, cols, transposed):
    blocks = []
    for tap in range(3):
        narrow = lax.broadcasted_iota(jnp.int32, (rows, cols), 1 if not transposed else 0)
        wide = lax.broadcasted_iota(jnp.int32, (rows, cols), 0 if not transposed else 1)
        blocks.append(jnp.where(wide == 2 * narrow + tap - 1, 1.0, 0.0).astype(jnp.bfloat16))
    return jnp.concatenate(blocks, axis=1)


def forward_taps(source_refs, kbig_ref, acc_ref, out_refs, picked_ref, first_tap):
    planes = len(source_refs)
    rows, chans, cols = source_refs[0].shape
    rows_out, cols_out = rows // 2, cols // 2
    share = out_refs[0].shape[1]
    sel = spread_matrix(cols, cols_out, False)
    for plane, source_ref in enumerate(source_refs):
        flat = source_ref[...].reshape(rows * chans, cols)
        chosen = jnp.dot(flat, sel, preferred_element_type=jnp.float32)
        picked_ref[plane] = chosen.astype(picked_ref.dtype).reshape(rows, chans, 3 * cols_out)
    kpart = kbig_ref[:, first_tap * 9 * chans:(first_tap + planes) * 9 * chans]
    zero = jnp.zeros((chans, cols_out), picked_ref.dtype)
    for i in range(rows_out):
        pieces = []
        for plane in range(planes):
            for row_tap in range(3):
                row = 2 * i + row_tap - 1
                for col_tap in range(3):
                    if row < 0:
                        pieces.append(zero)
                    else:
                        pieces.append(picked_ref[plane, row, :, col_tap * cols_out:(col_tap + 1) * cols_out])
        stacked = jnp.concatenate(pieces, axis=0)
        result = jnp.dot(kpart, stacked, preferred_element_type=jnp.float32)
        if acc_ref is not None:
            result = acc_ref[i] + result
        if len(out_refs) == 1 and share == result.shape[0]:
            out_refs[0][i] = result
        else:
            for k, out_ref in enumerate(out_refs):
                out_ref[i] = result[k * share:(k + 1) * share]


def forward_local_rows(vol_ref, kbig_ref, acc_ref, picked_ref):
    forward_taps([vol_ref.at[0], vol_ref.at[1]], kbig_ref, None, [acc_ref], picked_ref, 1)


def forward_halo_rows(halo_ref, acc_ref, kbig_ref, *refs):
    out_refs, picked_ref = refs[:-1], refs[-1]
    forward_taps([halo_ref], kbig_ref, acc_ref, list(out_refs), picked_ref, 0)


def forward_partial(halo, vol, kernel, groups):
    planes, rows, chans, cols = vol.shape
    taps, _, chans_out = kernel.shape
    rows_out, cols_out = rows // 2, cols // 2
    share = chans_out // groups
    kbig = jnp.transpose(kernel, (2, 0, 1)).reshape(chans_out, taps * chans)
    vmem = pl.BlockSpec(memory_space=pltpu.VMEM)
    per_plane = 2 * rows * chans * cols * 3 * cols_out + 2 * rows_out * chans_out * 9 * chans * cols_out
    acc = pl.pallas_call(
        forward_local_rows,
        out_shape=jax.ShapeDtypeStruct((rows_out, chans_out, cols_out), jnp.float32),
        in_specs=[vmem] * 2,
        out_specs=vmem,
        scratch_shapes=[pltpu.VMEM((planes, rows, chans, 3 * cols_out), vol.dtype)],
        cost_estimate=pl.CostEstimate(flops=planes * per_plane, bytes_accessed=2 * vol.size + 4 * rows_out * chans_out * cols_out, transcendentals=0),
    )(vol, kbig)
    return pl.pallas_call(
        forward_halo_rows,
        out_shape=[jax.ShapeDtypeStruct((rows_out, share, cols_out), jnp.float32)] * groups,
        in_specs=[vmem] * 3,
        out_specs=[vmem] * groups,
        scratch_shapes=[pltpu.VMEM((1, rows, chans, 3 * cols_out), vol.dtype)],
        cost_estimate=pl.CostEstimate(flops=per_plane, bytes_accessed=2 * halo.size + 8 * rows_out * chans_out * cols_out, transcendentals=0),
    )(pltpu.with_memory_space_constraint(halo, pltpu.MemorySpace.VMEM), acc, kbig)


def backward_rows(*refs):
    groups = (len(refs) - 3)
    cot_refs, k_ref, out_ref, up_ref = refs[:groups], refs[groups], refs[groups + 1], refs[groups + 2]
    planes, rows_out, share, cols_out = cot_refs[0].shape
    rows = out_ref.shape[1]
    cols = out_ref.shape[3]
    tsel = spread_matrix(cols_out, cols, True)
    for k, cot_ref in enumerate(cot_refs):
        flat = cot_ref[...].reshape(planes * rows_out * share, cols_out)
        spread = jnp.dot(flat, tsel, preferred_element_type=jnp.float32)
        up_ref[:, :, k * share:(k + 1) * share, :] = spread.astype(up_ref.dtype).reshape(planes, rows_out, share, 3 * cols)
    for depth in range(2):
        sources = [(1, 0)] if depth == 0 else [(2, 0), (0, 1)]
        for row in range(rows):
            weights, values = [], []
            for depth_tap, plane in sources:
                for row_tap in range(3):
                    if (row + 1 - row_tap) % 2:
                        continue
                    i = (row + 1 - row_tap) // 2
                    if not 0 <= i < rows_out:
                        continue
                    for col_tap in range(3):
                        weights.append(k_ref[9 * depth_tap + 3 * row_tap + col_tap])
                        values.append(up_ref[plane, i, :, col_tap * cols:(col_tap + 1) * cols])
            lhs = jnp.concatenate(weights, axis=1)
            rhs = jnp.concatenate(values, axis=0)
            out_ref[depth, row] = jnp.dot(lhs, rhs, preferred_element_type=jnp.float32).astype(out_ref.dtype)


def backward_grad(pieces, kernel):
    planes, rows_out, share, cols_out = pieces[0].shape
    chans_out = share * len(pieces)
    taps, chans, _ = kernel.shape
    rows, cols = 2 * rows_out, 2 * cols_out
    flops = 2 * planes * rows_out * chans_out * cols_out * 3 * cols + 2 * 2 * rows * chans * 9 * chans_out * cols
    return pl.pallas_call(
        backward_rows,
        out_shape=jax.ShapeDtypeStruct((2, rows, chans, cols), kernel.dtype),
        in_specs=[pl.BlockSpec(memory_space=pltpu.VMEM)] * (len(pieces) + 1),
        out_specs=pl.BlockSpec(memory_space=pltpu.VMEM),
        scratch_shapes=[pltpu.VMEM((planes, rows_out, chans_out, 3 * cols), kernel.dtype)],
        cost_estimate=pl.CostEstimate(flops=flops, bytes_accessed=2 * planes * rows_out * chans_out * cols_out + 2 * 2 * rows * chans * cols, transcendentals=0),
    )(*pieces, kernel)


def sum_parts(*refs):
    out_ref = refs[-1]
    total = refs[0][...]
    for ref in refs[1:-1]:
        total = total + ref[...]
    out_ref[...] = total.astype(out_ref.dtype)


def chan_shift(block, shift):
    size = lax.axis_size("chan")
    return lax.ppermute(block, "chan", [(i, (i + shift) % size) for i in range(size)])


def per_device(volume, kernel, cotangent):
    count, planes_in, rows_in, chans_in, cols_in = volume.shape
    planes_out = planes_in // 2
    rows_out = rows_in // 2
    cols_out = cols_in // 2
    chans_out = kernel.shape[2]
    groups = lax.axis_size("chan")
    share = chans_out // groups
    me = lax.axis_index("chan")
    kernel = jnp.roll(kernel, -me * share, axis=2)
    below = from_behind(volume[:, -1:], "space", 1)
    chunks = forward_partial(below[0, 0], volume[0], kernel, groups)
    pair = jnp.concatenate([cotangent, from_behind(cotangent, "space", -1)], axis=1)
    chunks, pair = lax.optimization_barrier((chunks, pair))
    parts = [chunks[0]] + [chan_shift(chunks[k], k) for k in range(1, groups)]
    response = pl.pallas_call(
        sum_parts,
        out_shape=jax.ShapeDtypeStruct(parts[0].shape, jnp.bfloat16),
        in_specs=[pl.BlockSpec(memory_space=pltpu.VMEM)] * groups,
        out_specs=pl.BlockSpec(memory_space=pltpu.VMEM),
    )(*[pltpu.with_memory_space_constraint(part, pltpu.MemorySpace.VMEM) for part in parts])
    response = response.reshape(count, planes_out, rows_out, share, cols_out)
    pieces = [pair[0]] + [chan_shift(pair[0], -k) for k in range(1, groups)]
    volume_grad = backward_grad(pieces, kernel).reshape(count, planes_in, rows_in, chans_in, cols_in)
    return (response, volume_grad)


def solution(mesh):
    placed = (
        P("dp", "space", None, "chan", None),
        P(None, "chan", None),
        P("dp", "space", None, "chan", None),
    )
    return jax.shard_map(
        per_device,
        mesh=mesh,
        in_specs=placed,
        out_specs=(P("dp", "space", None, "chan", None), P("dp", "space", None, "chan", None)),
        check_vma=False,
    )
```
